128 devices in a mesh: req: 128 (over y, z, x, core).
Axes of the slice: x: 4, y: 4, z: 4, core: 2. Of those that a mesh axis runs over, the one named last changes fastest.
Arguments:
- hidden: bfloat16 [32768, 1024], P('req'), may hold values from -6 to 6
- draft_query: bfloat16 [32768, 1024], P('req'), may hold values from -204 to 204
- draft_key: bfloat16 [32768, 1024], P('req'), may hold values from -6 to 6
- draft_value: bfloat16 [32768, 1024], P('req'), may hold values from -6 to 6
- cache_keys: bfloat16 [12288, 16, 1024], P('req'), may hold values from -6 to 6
- cache_values: bfloat16 [12288, 16, 1024], P('req'), may hold values from -6 to 6
- page_target: int32 [12288, 1], P('req'), may hold values from 0 to 127; in each aligned block of 96 rows (0 to 95, 96 to 191, ...) at most 2 rows name the same one
- page_slot: int32 [12288], P('req'), may hold values from 0 to 3
- page_fill: int32 [12288], P('req'), may hold values from 1 to 16
- tree_parent: int32 [512, 64], P('req'), may hold values from -1 to 62, as said below
- tree_size: int32 [512], P('req'), may hold values from 32 to 64
- accepted_leaf: int32 [512], P('req'), may hold values from 0 to 63
- w_attn_out: bfloat16 [1024, 1024], replicated, may hold values from -0.1875 to 0.1875
- ln_gain: bfloat16 [1024], replicated, may hold values from 0.099609375 to 1.8984375
- w_in: bfloat16 [1024, 5248], replicated, may hold values from -0.1875 to 0.1875
- w_out: bfloat16 [2624, 1024], replicated, may hold values from -0.125 to 0.125
Outputs:
- layer_out: bfloat16 [32768, 1024], P('req')
- kept_keys: bfloat16 [32768, 1024], P('req')
- kept_values: bfloat16 [32768, 1024], P('req')
The draws below stay inside these ranges and needn't reach their ends.
Inputs may be any that keep to these rules, and one draw needn't show every extreme that they name: `page_target`: among the 96 pages of one device each target device is named at most 2 times, a bound that some block reaches. `tree_parent`: slot 0 of every tree has parent -1; slot i > 0 has a parent below i.
All inputs are finite; a program needn't handle non-finite values.
Results may differ from the reference program's by a relative error of at most 0.011.
Values may be sent and summed in bfloat16 or wider, within the bound.
No kernel may reach another device: no remote copies, remote signals or barrier semaphores. Data moves between devices by JAX's collectives and lax.ppermute only.
A program may use at most 192 MiB of HBM per device.

```python
import math
import jax
import jax.numpy as jnp
import numpy as np
from jax import lax

D = 1024
HEADS = 16
FF = 2624
TREE = 64
PAGE = 16
REQ_DEV = 4
PAGES_DEV = 96
CAP = 2
REQS = 512
TOKENS = 32768
PAGES = 12288
N_REQ = 128


def draw_draft_query(key, part):
    values = jnp.clip(jax.random.normal(key, (TOKENS, D), jnp.float32), -6.0, 6.0)
    return values.astype(jnp.bfloat16)


def draw_tree_parent(key, part):
    slots = jnp.arange(TREE, dtype=jnp.int32)[None, :]
    request_rows = jnp.arange(REQS, dtype=jnp.int32)[:, None]
    raw = jax.random.randint(key, (REQS, TREE), 0, 1 << 20)
    parent = raw % jnp.maximum(slots, 1)
    parent = jnp.where((request_rows == 0) & (slots == TREE - 1), TREE - 2, parent)
    return jnp.where(slots == 0, -1, parent).astype(jnp.int32)


def with_ends(values, stream_key, low, largest):
    spot = [jax.random.randint(jax.random.fold_in(stream_key, axis), (), 0, length) for axis, length in enumerate(values.shape)]
    widest = values.shape.index(max(values.shape))
    beside = spot[:widest] + [(spot[widest] + 1) % values.shape[widest]] + spot[widest + 1:]
    return values.at[tuple(spot)].set(low).at[tuple(beside)].set(largest)


def block_scale(rng, shape, cuts, smallest, largest):
    def one(position, blocks):
        steps = jax.random.uniform(jax.random.fold_in(jax.random.fold_in(rng, 6), position), (blocks,), jnp.float32, smallest / len(cuts), largest / len(cuts))
        return jnp.repeat(jnp.exp(steps), shape[position] // blocks).reshape((-1,) + (1,) * (len(shape) - position - 1))

    factor_of = one(*cuts[0])
    for cut in cuts[1:]:
        factor_of = factor_of * one(*cut)
    return factor_of


def shared_out(rng, own, number, rows, count, top, limit, lean):
    ranking = jax.random.permutation(rng, count)
    crowded, usual = portions_of(count, rows * top, limit, lean, True), portions_of(count, rows * top, limit, lean, False)
    places = jnp.arange(count)

    def named(tallies, offset_by):
        used = int((tallies > 0).sum())
        fixed = max(1, used // 4)
        passed = fixed + (places - fixed + offset_by * (used - fixed)) % max(1, count - fixed)
        return jnp.zeros((count,), jnp.int32).at[ranking[jnp.where(places < fixed, places, passed)]].set(jnp.asarray(tallies, jnp.int32))

    tallies = jnp.where(number % 4 == 0, named(crowded, number // 4), named(usual, number - number // 4 - 1))
    mixed = jax.random.permutation(jax.random.fold_in(own, 3), count)
    giver, sink = mixed[0:count // 2 * 2:2], mixed[1:count // 2 * 2:2]
    margin = jnp.minimum(tallies[giver] - 1, limit - tallies[sink]) // 2
    margin = jnp.where((giver == ranking[0]) | (sink == ranking[0]) | (tallies[sink] == 0), 0, jnp.maximum(margin, 0))
    passed = jax.random.randint(jax.random.fold_in(own, 4), (count // 2,), 0, 1 << 20) % (margin + 1)
    tallies = tallies.at[giver].add(-passed).at[sink].add(passed)
    members = jnp.searchsorted(jnp.cumsum(tallies), jnp.arange(rows * top), side="right").astype(jnp.int32)
    listing = members.reshape(top, rows).T
    listing = listing[jax.random.permutation(jax.random.fold_in(own, 1), rows)]
    offset_by = jax.random.randint(jax.random.fold_in(own, 2), (rows, 1), 0, top)
    return jnp.take_along_axis(listing, (jnp.arange(top)[None, :] + offset_by) % top, axis=1)


def portions_of(amount, total, limit, skew, full):
    weights = [(1 << 20) // math.isqrt(rank ** skew) + 1 for rank in range(1, amount + 1)]
    largest = limit if full else min(limit, max(-(-total // amount), total * weights[0] // sum(weights)))
    least = 1 if total - largest >= amount - 1 else 0
    holding, rest = [largest] + [least] * (amount - 1), total - largest - least * (amount - 1)
    while rest > 0:
        movable = [i for i in range(1, amount) if holding[i] < largest] or [i for i in range(1, amount) if holding[i] < limit]
        whole, left = sum([weights[i] for i in movable]), rest
        for i in movable:
            addition = min(limit - holding[i], max(1, left * weights[i] // whole), rest)
            holding[i] = holding[i] + addition
            rest = rest - addition
    return np.array(holding)


def bell_draw(stream_key, dims, deviation, most, cuts=(), kind=jnp.bfloat16):
    gain = block_scale(stream_key, dims, cuts, -0.22, 0.18) if cuts else 1.0
    entries = jax.random.normal(stream_key, dims, jnp.float32) * deviation * gain
    return jnp.minimum(jnp.maximum(entries, -most), most).astype(kind)


def setup_inputs(seed: int = 0) -> dict:
    streams_of = jax.random.split(jax.random.key(seed), 17)
    hidden = bell_draw(streams_of[0], (TOKENS, D), 1.0, 6.0, ((0, 128),))
    draft_query = draw_draft_query(jax.random.fold_in(streams_of[16], 71), 0)
    draft_key = bell_draw(streams_of[2], (TOKENS, D), 1.0, 6.0, ((0, 128),))
    draft_value = bell_draw(streams_of[3], (TOKENS, D), 1.0, 6.0, ((0, 128),))
    cache_keys = bell_draw(streams_of[4], (PAGES, PAGE, D), 1.0, 6.0, ((0, 128),))
    cache_values = bell_draw(streams_of[5], (PAGES, PAGE, D), 1.0, 6.0, ((0, 128),))
    page_target_keys = jax.random.split(jax.random.fold_in(streams_of[6], 1), PAGES // PAGES_DEV)
    page_target_turns = jax.random.permutation(jax.random.fold_in(streams_of[6], 3), PAGES // PAGES_DEV)
    page_target = jax.vmap(lambda own, number: shared_out(jax.random.fold_in(streams_of[6], 2), own, number, PAGES_DEV, N_REQ, 1, CAP, 2))(page_target_keys, page_target_turns).reshape((PAGES, 1))
    page_slot = with_ends(jax.random.randint(streams_of[7], (PAGES,), 0, REQ_DEV), jax.random.fold_in(streams_of[7], 1), 0, REQ_DEV - 1).astype(jnp.int32)
    page_fill = with_ends(jax.random.randint(streams_of[8], (PAGES,), 1, PAGE + 1), jax.random.fold_in(streams_of[8], 1), 1, PAGE).astype(jnp.int32)
    tree_parent = draw_tree_parent(jax.random.fold_in(streams_of[16], 71), 0)
    tree_size = with_ends(jax.random.randint(streams_of[10], (REQS,), TREE // 2, TREE + 1), jax.random.fold_in(streams_of[10], 1), TREE // 2, TREE).astype(jnp.int32)
    accepted_leaf = with_ends(jax.random.randint(streams_of[11], (REQS,), 0, TREE), jax.random.fold_in(streams_of[11], 1), 0, TREE - 1).astype(jnp.int32)
    w_attn_out = bell_draw(streams_of[12], (D, D), D ** -0.5, 0.1875)
    ln_gain = jnp.clip(1.0 + 0.18 * jax.random.normal(streams_of[13], (D,), jnp.float32), 0.099609375, 1.8984375).astype(jnp.bfloat16)
    w_in = bell_draw(streams_of[14], (D, 2 * FF), D ** -0.5, 0.1875)
    w_out = bell_draw(streams_of[15], (FF, D), FF ** -0.5, 0.125)
    return dict(hidden=hidden, draft_query=draft_query, draft_key=draft_key, draft_value=draft_value, cache_keys=cache_keys, cache_values=cache_values, page_target=page_target, page_slot=page_slot, page_fill=page_fill, tree_parent=tree_parent, tree_size=tree_size, accepted_leaf=accepted_leaf, w_attn_out=w_attn_out, ln_gain=ln_gain, w_in=w_in, w_out=w_out)


def ancestor_closure(tree_parent):
    width = tree_parent.shape[1]
    ident = jnp.eye(width, dtype=jnp.float32)
    ancestors = (tree_parent[:, :, None] == jnp.arange(width, dtype=jnp.int32)[None, None, :]).astype(jnp.float32) + ident
    for repeat in range((width - 1).bit_length()):
        ancestors = jnp.minimum(jnp.einsum('rij,rjk->rik', ancestors, ancestors, precision=lax.Precision.HIGHEST), 1.0)
    return ancestors

def rotate_positions(values, positions, heads):
    rows, width = values.shape
    head_size = width // heads
    half = head_size // 2
    inverse = jnp.power(160000.0, -(2.0 * jnp.arange(half, dtype=jnp.float32)) / head_size)
    angle = positions.astype(jnp.float32)[:, None] * inverse[None, :]
    cosine = jnp.cos(angle)[:, None, :]
    sine = jnp.sin(angle)[:, None, :]
    shaped = values.astype(jnp.float32).reshape(rows, heads, head_size)
    first = shaped[..., :half]
    second = shaped[..., half:]
    turned = jnp.concatenate([first * cosine - second * sine, second * cosine + first * sine], axis=-1)
    return turned.reshape(rows, width).astype(jnp.bfloat16)

def attend_tree(queries, keys, values, key_mask, heads):
    rows, width = queries.shape
    head_size = width // heads
    scale = 1.0 / head_size ** 0.5
    query3 = queries.reshape(rows, heads, head_size)
    key3 = keys.reshape(keys.shape[0], heads, head_size)
    value3 = values.reshape(values.shape[0], heads, head_size)

    def one_head(head):
        query_h = lax.dynamic_index_in_dim(query3, head, 1, keepdims=False)
        key_h = lax.dynamic_index_in_dim(key3, head, 1, keepdims=False)
        value_h = lax.dynamic_index_in_dim(value3, head, 1, keepdims=False)
        scores = jnp.dot(query_h, key_h.T, preferred_element_type=jnp.float32) * scale
        scores = jnp.where(key_mask, scores, -1e+30)
        row_max = lax.optimization_barrier(jnp.max(scores, axis=1, keepdims=True))
        weights = jnp.where(key_mask, jnp.exp(scores - row_max), 0.0)
        probs = (weights / lax.optimization_barrier(jnp.sum(weights, axis=1, keepdims=True))).astype(jnp.bfloat16)
        return jnp.dot(probs, value_h, preferred_element_type=jnp.float32)
    context = lax.map(one_head, jnp.arange(heads, dtype=jnp.int32))
    return jnp.transpose(context, (1, 0, 2)).reshape(rows, width).astype(jnp.bfloat16)

def feed_forward(rows_in, ln_gain, w_in, w_out):
    inner = w_out.shape[0]
    floats = rows_in.astype(jnp.float32)
    mean_value = lax.optimization_barrier(jnp.mean(floats, axis=1, keepdims=True))
    centred = floats - mean_value
    variance = lax.optimization_barrier(jnp.mean(centred * centred, axis=1, keepdims=True))
    normed = (centred * lax.rsqrt(variance + 1e-05) * ln_gain.astype(jnp.float32)[None, :]).astype(jnp.bfloat16)
    both = jnp.dot(normed, w_in, preferred_element_type=jnp.float32)
    middle = (jax.nn.gelu(both[:, :inner], approximate=False) * both[:, inner:]).astype(jnp.bfloat16)
    return jnp.dot(middle, w_out, preferred_element_type=jnp.float32).astype(jnp.bfloat16)

def verify_layer(hidden, draft_query, draft_key, draft_value, recv_keys, recv_values, recv_fill, recv_owner, tree_parent, tree_size, accepted_leaf, w_attn_out, ln_gain, w_in, w_out):
    requests, width = tree_parent.shape
    rows = requests * width
    page_len = recv_keys.shape[0] // recv_fill.shape[0]
    ancestors = ancestor_closure(tree_parent)
    depth = (lax.optimization_barrier(jnp.sum(ancestors, axis=2)) - 1.0).astype(jnp.int32)
    request_ids = jnp.arange(requests, dtype=jnp.int32)
    cache_len = lax.optimization_barrier(jnp.sum(jnp.where(recv_owner[None, :] == request_ids[:, None], recv_fill[None, :], 0), axis=1)).astype(jnp.int32)
    positions = (cache_len[:, None] + depth).reshape(rows)
    query_rot = rotate_positions(draft_query, positions, HEADS)
    key_rot = rotate_positions(draft_key, positions, HEADS)
    key_owner = jnp.where(jnp.arange(page_len, dtype=jnp.int32)[None, :] < recv_fill[:, None], recv_owner[:, None], -1).reshape(-1)
    query_owner = jnp.arange(rows, dtype=jnp.int32) // width
    cache_mask = query_owner[:, None] == key_owner[None, :]
    tree_mask = (ancestors[:, :, None, :] * jnp.eye(requests, dtype=jnp.float32)[:, None, :, None]).reshape(rows, rows) > 0.5
    key_mask = jnp.concatenate([cache_mask, tree_mask], axis=1)
    all_keys = jnp.concatenate([recv_keys, key_rot], axis=0)
    all_values = jnp.concatenate([recv_values, draft_value], axis=0)
    context = attend_tree(query_rot, all_keys, all_values, key_mask, HEADS)
    attended = (hidden.astype(jnp.float32) + jnp.dot(context, w_attn_out, preferred_element_type=jnp.float32)).astype(jnp.bfloat16)
    alive_mask = (jnp.arange(width, dtype=jnp.int32)[None, :] < tree_size[:, None]).reshape(rows)
    ffn_out = feed_forward(attended, ln_gain, w_in, w_out)
    layer_out = jnp.where(alive_mask[:, None], attended.astype(jnp.float32) + ffn_out.astype(jnp.float32), 0.0).astype(jnp.bfloat16)
    leaf_index = jnp.minimum(accepted_leaf, tree_size - 1)
    leaf_onehot = (jnp.arange(width, dtype=jnp.int32)[None, :] == leaf_index[:, None]).astype(jnp.float32)
    path = jnp.einsum('ri,rij->rj', leaf_onehot, ancestors, precision=lax.Precision.HIGHEST)
    select = path[:, None, :] * (depth[:, None, :] == jnp.arange(width, dtype=jnp.int32)[None, :, None]).astype(jnp.float32)
    kept_keys = jnp.einsum('rkj,rjd->rkd', select, key_rot.reshape(requests, width, -1).astype(jnp.float32), precision=lax.Precision.HIGHEST)
    kept_values = jnp.einsum('rkj,rjd->rkd', select, draft_value.reshape(requests, width, -1).astype(jnp.float32), precision=lax.Precision.HIGHEST)
    return (layer_out, kept_keys.reshape(rows, -1).astype(jnp.bfloat16), kept_values.reshape(rows, -1).astype(jnp.bfloat16))

def reference(hidden, draft_query, draft_key, draft_value, cache_keys, cache_values, page_target, page_slot, page_fill, tree_parent, tree_size, accepted_leaf, w_attn_out, ln_gain, w_in, w_out):
    per_device = REQ_DEV * TREE
    target = page_target[:, 0]
    keys_pad = jnp.concatenate([cache_keys, jnp.zeros((1, PAGE, D), cache_keys.dtype)], axis=0)
    values_pad = jnp.concatenate([cache_values, jnp.zeros((1, PAGE, D), cache_values.dtype)], axis=0)
    fill_pad = jnp.concatenate([page_fill, jnp.zeros((1,), jnp.int32)], axis=0)
    slot_pad = jnp.concatenate([page_slot, jnp.zeros((1,), jnp.int32)], axis=0)

    def one_device(device):
        picked = jnp.nonzero(target == device, size=N_REQ * CAP, fill_value=PAGES)[0].astype(jnp.int32)
        recv_keys = keys_pad[picked].reshape(-1, D)
        recv_values = values_pad[picked].reshape(-1, D)
        start = (device * per_device).astype(jnp.int32)
        req_start = (device * REQ_DEV).astype(jnp.int32)
        return verify_layer(lax.dynamic_slice_in_dim(hidden, start, per_device, 0), lax.dynamic_slice_in_dim(draft_query, start, per_device, 0), lax.dynamic_slice_in_dim(draft_key, start, per_device, 0), lax.dynamic_slice_in_dim(draft_value, start, per_device, 0), recv_keys, recv_values, fill_pad[picked], slot_pad[picked], lax.dynamic_slice_in_dim(tree_parent, req_start, REQ_DEV, 0), lax.dynamic_slice_in_dim(tree_size, req_start, REQ_DEV, 0), lax.dynamic_slice_in_dim(accepted_leaf, req_start, REQ_DEV, 0), w_attn_out, ln_gain, w_in, w_out)
    layer_out, kept_keys, kept_values = lax.map(one_device, jnp.arange(N_REQ, dtype=jnp.int32))
    return (layer_out.reshape(TOKENS, D), kept_keys.reshape(TOKENS, D), kept_values.reshape(TOKENS, D))
```

```python
import functools

import jax
import jax.numpy as jnp
from jax import lax
from jax.experimental import pallas as pl
from jax.experimental.pallas import tpu as pltpu
from jax.sharding import PartitionSpec as P

HEADS = 16


def ancestor_closure(tree_parent):
    width = tree_parent.shape[1]
    ident = jnp.eye(width, dtype=jnp.float32)
    ancestors = (
        tree_parent[:, :, None] == jnp.arange(width, dtype=jnp.int32)[None, None, :]
    ).astype(jnp.float32) + ident
    for repeat in range((width - 1).bit_length()):
        ancestors = jnp.minimum(
            jnp.einsum("rij,rjk->rik", ancestors, ancestors, precision=lax.Precision.HIGHEST), 1.0
        )
    return ancestors


def rotate_positions(values, positions, heads):
    rows, width = values.shape
    head_size = width // heads
    half = head_size // 2
    inverse = jnp.power(160000.0, -(2.0 * jnp.arange(half, dtype=jnp.float32)) / head_size)
    angle = positions.astype(jnp.float32)[:, None] * inverse[None, :]
    cosine = jnp.cos(angle)[:, None, :]
    sine = jnp.sin(angle)[:, None, :]
    shaped = values.astype(jnp.float32).reshape(rows, heads, head_size)
    first = shaped[..., :half]
    second = shaped[..., half:]
    turned = jnp.concatenate(
        [first * cosine - second * sine, second * cosine + first * sine], axis=-1
    )
    return turned.reshape(rows, width).astype(jnp.bfloat16)


def _attend_kernel(q_ref, kc_ref, vc_ref, kd_ref, vd_ref, kown_ref, tmask_ref, o_ref, *,
                   tree_width, head_size, scale):
    rows, lanes = q_ref.shape
    q = q_ref[...]
    kc = kc_ref[...].reshape(-1, lanes)
    vc = vc_ref[...].reshape(-1, lanes)
    kd = kd_ref[...]
    vd = vd_ref[...]
    lane = lax.broadcasted_iota(jnp.int32, (1, lanes), 1)
    qown = lax.broadcasted_iota(jnp.int32, (rows, 1), 0) // tree_width
    cmask = qown == kown_ref[...]
    tmask = tmask_ref[...] > 0.5
    dims = (((1,), (1,)), ((), ()))
    outs = []
    for part in range(lanes // head_size):
        sel = (lane >= part * head_size) & (lane < (part + 1) * head_size)
        qh = jnp.where(sel, q, jnp.zeros((), q.dtype))
        sc = lax.dot_general(qh, kc, dims, preferred_element_type=jnp.float32) * scale
        sd = lax.dot_general(qh, kd, dims, preferred_element_type=jnp.float32) * scale
        sc = jnp.where(cmask, sc, -1e30)
        sd = jnp.where(tmask, sd, -1e30)
        top = jnp.maximum(jnp.max(sc, axis=1, keepdims=True), jnp.max(sd, axis=1, keepdims=True))
        pc = jnp.where(cmask, jnp.exp(sc - top), 0.0)
        pd = jnp.where(tmask, jnp.exp(sd - top), 0.0)
        inv = 1.0 / (jnp.sum(pc, axis=1, keepdims=True) + jnp.sum(pd, axis=1, keepdims=True))
        ctx = jnp.dot((pc * inv).astype(jnp.bfloat16), vc, preferred_element_type=jnp.float32)
        ctx = ctx + jnp.dot((pd * inv).astype(jnp.bfloat16), vd, preferred_element_type=jnp.float32)
        outs.append((sel, ctx))
    result = outs[0][1]
    for sel, ctx in outs[1:]:
        result = jnp.where(sel, ctx, result)
    o_ref[...] = result.astype(o_ref.dtype)


def attend(query_rot, recv, key_rot, draft_value, key_owner, tree_mask, tree_width):
    rows, width = query_rot.shape
    head_size = width // HEADS
    lanes = 128
    slots, _, page_len, _ = recv.shape
    kernel = functools.partial(
        _attend_kernel, tree_width=tree_width, head_size=head_size, scale=1.0 / head_size**0.5
    )
    return pl.pallas_call(
        kernel,
        grid=(width // lanes,),
        in_specs=[
            pl.BlockSpec((rows, lanes), lambda h: (0, h)),
            pl.BlockSpec((slots, None, page_len, lanes), lambda h: (0, 0, 0, h)),
            pl.BlockSpec((slots, None, page_len, lanes), lambda h: (0, 1, 0, h)),
            pl.BlockSpec((rows, lanes), lambda h: (0, h)),
            pl.BlockSpec((rows, lanes), lambda h: (0, h)),
            pl.BlockSpec((1, slots * page_len), lambda h: (0, 0)),
            pl.BlockSpec((rows, rows), lambda h: (0, 0)),
        ],
        out_specs=pl.BlockSpec((rows, lanes), lambda h: (0, h)),
        out_shape=jax.ShapeDtypeStruct((rows, width), jnp.bfloat16),
        compiler_params=pltpu.CompilerParams(vmem_limit_bytes=60 * 1024 * 1024),
    )(query_rot, recv, recv, key_rot, draft_value, key_owner, tree_mask)


def feed_forward(rows_in, ln_gain, w_in, w_out):
    inner = w_out.shape[0]
    floats = rows_in.astype(jnp.float32)
    mean_value = jnp.mean(floats, axis=1, keepdims=True)
    centred = floats - mean_value
    variance = jnp.mean(centred * centred, axis=1, keepdims=True)
    normed = (centred * lax.rsqrt(variance + 1e-05) * ln_gain.astype(jnp.float32)[None, :]).astype(
        jnp.bfloat16
    )
    both = jnp.dot(normed, w_in, preferred_element_type=jnp.float32)
    middle = (jax.nn.gelu(both[:, :inner], approximate=False) * both[:, inner:]).astype(
        jnp.bfloat16
    )
    return jnp.dot(middle, w_out, preferred_element_type=jnp.float32).astype(jnp.bfloat16)


def local(
    hidden,
    draft_query,
    draft_key,
    draft_value,
    cache_keys,
    cache_values,
    page_target,
    page_slot,
    page_fill,
    tree_parent,
    tree_size,
    accepted_leaf,
    w_attn_out,
    ln_gain,
    w_in,
    w_out,
):
    devices = lax.axis_size("req")
    pages_here, page_len, width = cache_keys.shape
    per_target = max(2, -(-pages_here // devices))
    target = page_target[:, 0]
    onehot = (target[:, None] == jnp.arange(devices, dtype=jnp.int32)[None, :]).astype(jnp.int32)
    within = jnp.sum(jnp.cumsum(onehot, axis=0) * onehot, axis=1) - 1
    dest_slot = target * per_target + within
    slot_count = devices * per_target
    matches = dest_slot[None, :] == jnp.arange(slot_count, dtype=jnp.int32)[:, None]
    filled = jnp.any(matches, axis=1)
    source = jnp.sum(
        jnp.where(matches, jnp.arange(pages_here, dtype=jnp.int32)[None, :], 0), axis=1
    )
    send_kv = jnp.stack([cache_keys[source], cache_values[source]], axis=1)
    send_meta = jnp.stack(
        [jnp.where(filled, page_fill[source], 0), page_slot[source]], axis=1
    ).reshape(devices, per_target * 2)
    recv_meta = lax.all_to_all(send_meta, "req", 0, 0, tiled=True).reshape(slot_count, 2)
    recv = lax.all_to_all(
        send_kv.reshape(devices, per_target * 2, page_len, width), "req", 0, 0, tiled=True
    ).reshape(slot_count, 2, page_len, width)
    recv_fill = recv_meta[:, 0]
    recv_owner = recv_meta[:, 1]
    requests, tree_width = tree_parent.shape
    rows = requests * tree_width
    ancestors = ancestor_closure(tree_parent)
    depth = (jnp.sum(ancestors, axis=2) - 1.0).astype(jnp.int32)
    request_ids = jnp.arange(requests, dtype=jnp.int32)
    cache_len = jnp.sum(
        jnp.where(recv_owner[None, :] == request_ids[:, None], recv_fill[None, :], 0), axis=1
    )
    positions = (cache_len[:, None] + depth).reshape(rows)
    query_rot = rotate_positions(draft_query, positions, HEADS)
    key_rot = rotate_positions(draft_key, positions, HEADS)
    key_owner = jnp.where(
        jnp.arange(page_len, dtype=jnp.int32)[None, :] < recv_fill[:, None], recv_owner[:, None], -1
    ).reshape(1, -1)
    tree_mask = (
        ancestors[:, :, None, :] * jnp.eye(requests, dtype=jnp.float32)[:, None, :, None]
    ).reshape(rows, rows)
    context = attend(query_rot, recv, key_rot, draft_value, key_owner, tree_mask, tree_width)
    attended = (
        hidden.astype(jnp.float32)
        + jnp.dot(context, w_attn_out, preferred_element_type=jnp.float32)
    ).astype(jnp.bfloat16)
    alive_mask = (jnp.arange(tree_width, dtype=jnp.int32)[None, :] < tree_size[:, None]).reshape(
        rows
    )
    ffn_out = feed_forward(attended, ln_gain, w_in, w_out)
    layer_out = jnp.where(
        alive_mask[:, None], attended.astype(jnp.float32) + ffn_out.astype(jnp.float32), 0.0
    ).astype(jnp.bfloat16)
    leaf_index = jnp.minimum(accepted_leaf, tree_size - 1)
    leaf_onehot = (jnp.arange(tree_width, dtype=jnp.int32)[None, :] == leaf_index[:, None]).astype(
        jnp.float32
    )
    path = jnp.einsum("ri,rij->rj", leaf_onehot, ancestors, precision=lax.Precision.HIGHEST)
    select = (
        path[:, None, :]
        * (depth[:, None, :] == jnp.arange(tree_width, dtype=jnp.int32)[None, :, None]).astype(
            jnp.float32
        )
    ).astype(jnp.bfloat16)
    kept_keys = jnp.einsum(
        "rkj,rjd->rkd",
        select,
        key_rot.reshape(requests, tree_width, width),
        preferred_element_type=jnp.float32,
    )
    kept_values = jnp.einsum(
        "rkj,rjd->rkd",
        select,
        draft_value.reshape(requests, tree_width, width),
        preferred_element_type=jnp.float32,
    )
    return (
        layer_out,
        kept_keys.reshape(rows, width).astype(jnp.bfloat16),
        kept_values.reshape(rows, width).astype(jnp.bfloat16),
    )


def solution(mesh):
    placed = (
        P("req", None),
        P("req", None),
        P("req", None),
        P("req", None),
        P("req", None, None),
        P("req", None, None),
        P("req", None),
        P("req"),
        P("req"),
        P("req", None),
        P("req"),
        P("req"),
        P(),
        P(),
        P(),
        P(),
    )
    return jax.shard_map(
        local,
        mesh=mesh,
        in_specs=placed,
        out_specs=(P("req", None), P("req", None), P("req", None)),
        check_vma=False,
    )
```

```python
import functools

import jax
import jax.numpy as jnp
from jax import lax
from jax.experimental import pallas as pl
from jax.experimental.pallas import tpu as pltpu
from jax.sharding import PartitionSpec as P

HEADS = 16


def ancestor_closure(tree_parent):
    width = tree_parent.shape[1]
    ident = jnp.eye(width, dtype=jnp.float32)
    ancestors = (
        tree_parent[:, :, None] == jnp.arange(width, dtype=jnp.int32)[None, None, :]
    ).astype(jnp.float32) + ident
    for repeat in range((width - 1).bit_length()):
        ancestors = jnp.minimum(
            jnp.einsum("rij,rjk->rik", ancestors, ancestors, precision=lax.Precision.HIGHEST), 1.0
        )
    return ancestors


def rotate_positions(values, positions, heads):
    rows, width = values.shape
    head_size = width // heads
    half = head_size // 2
    inverse = jnp.power(160000.0, -(2.0 * jnp.arange(half, dtype=jnp.float32)) / head_size)
    angle = positions.astype(jnp.float32)[:, None] * inverse[None, :]
    cosine = jnp.cos(angle)[:, None, :]
    sine = jnp.sin(angle)[:, None, :]
    shaped = values.astype(jnp.float32).reshape(rows, heads, head_size)
    first = shaped[..., :half]
    second = shaped[..., half:]
    turned = jnp.concatenate(
        [first * cosine - second * sine, second * cosine + first * sine], axis=-1
    )
    return turned.reshape(rows, width).astype(jnp.bfloat16)


def _probs_kernel(q_ref, kc_ref, kd_ref, kown_ref, tmask_ref, pc_ref, pd_ref, *,
                  tree_width, head_size, scale):
    rows, lanes = q_ref.shape
    q = q_ref[...]
    kc = kc_ref[...].reshape(-1, lanes)
    kd = kd_ref[...]
    lane = lax.broadcasted_iota(jnp.int32, (1, lanes), 1)
    qown = lax.broadcasted_iota(jnp.int32, (rows, 1), 0) // tree_width
    cmask = qown == kown_ref[...]
    tmask = tmask_ref[...] > 0.5
    dims = (((1,), (1,)), ((), ()))
    for part in range(lanes // head_size):
        sel = (lane >= part * head_size) & (lane < (part + 1) * head_size)
        qh = jnp.where(sel, q, jnp.zeros((), q.dtype))
        sc = lax.dot_general(qh, kc, dims, preferred_element_type=jnp.float32) * scale
        sd = lax.dot_general(qh, kd, dims, preferred_element_type=jnp.float32) * scale
        sc = jnp.where(cmask, sc, -1e30)
        sd = jnp.where(tmask, sd, -1e30)
        top = jnp.maximum(jnp.max(sc, axis=1, keepdims=True), jnp.max(sd, axis=1, keepdims=True))
        pc = jnp.exp(sc - top)
        pd = jnp.exp(sd - top)
        inv = 1.0 / (jnp.sum(pc, axis=1, keepdims=True) + jnp.sum(pd, axis=1, keepdims=True))
        pc_ref[part] = (pc * inv).astype(pc_ref.dtype)
        pd_ref[part] = (pd * inv).astype(pd_ref.dtype)


def _context_kernel(pc_ref, pd_ref, vc_ref, vd_ref, o_ref, *, head_size):
    rows, lanes = o_ref.shape
    vc = vc_ref[...].reshape(-1, lanes)
    vd = vd_ref[...]
    lane = lax.broadcasted_iota(jnp.int32, (1, lanes), 1)
    result = None
    for part in range(lanes // head_size):
        ctx = jnp.dot(pc_ref[part], vc, preferred_element_type=jnp.float32)
        ctx = ctx + jnp.dot(pd_ref[part], vd, preferred_element_type=jnp.float32)
        if result is None:
            result = ctx
        else:
            sel = (lane >= part * head_size) & (lane < (part + 1) * head_size)
            result = jnp.where(sel, ctx, result)
    o_ref[...] = result.astype(o_ref.dtype)


def attend(query_rot, recv_k, recv_v, key_rot, draft_value, key_owner, tree_mask, tree_width):
    rows, width = query_rot.shape
    head_size = width // HEADS
    lanes = 128
    per = lanes // head_size
    groups = width // lanes
    slots, page_len, _ = recv_k.shape
    keys = slots * page_len
    params = pltpu.CompilerParams(vmem_limit_bytes=60 * 1024 * 1024)
    probs_c, probs_d = pl.pallas_call(
        functools.partial(
            _probs_kernel, tree_width=tree_width, head_size=head_size, scale=1.0 / head_size**0.5
        ),
        grid=(groups,),
        in_specs=[
            pl.BlockSpec((rows, lanes), lambda h: (0, h)),
            pl.BlockSpec((slots, page_len, lanes), lambda h: (0, 0, h)),
            pl.BlockSpec((rows, lanes), lambda h: (0, h)),
            pl.BlockSpec((1, keys), lambda h: (0, 0)),
            pl.BlockSpec((rows, rows), lambda h: (0, 0)),
        ],
        out_specs=[
            pl.BlockSpec((None, per, rows, keys), lambda h: (h, 0, 0, 0)),
            pl.BlockSpec((None, per, rows, rows), lambda h: (h, 0, 0, 0)),
        ],
        out_shape=[
            jax.ShapeDtypeStruct((groups, per, rows, keys), jnp.bfloat16),
            jax.ShapeDtypeStruct((groups, per, rows, rows), jnp.bfloat16),
        ],
        compiler_params=params,
    )(query_rot, recv_k, key_rot, key_owner, tree_mask)
    return pl.pallas_call(
        functools.partial(_context_kernel, head_size=head_size),
        grid=(groups,),
        in_specs=[
            pl.BlockSpec((None, per, rows, keys), lambda h: (h, 0, 0, 0)),
            pl.BlockSpec((None, per, rows, rows), lambda h: (h, 0, 0, 0)),
            pl.BlockSpec((slots, page_len, lanes), lambda h: (0, 0, h)),
            pl.BlockSpec((rows, lanes), lambda h: (0, h)),
        ],
        out_specs=pl.BlockSpec((rows, lanes), lambda h: (0, h)),
        out_shape=jax.ShapeDtypeStruct((rows, width), jnp.bfloat16),
        compiler_params=params,
    )(probs_c, probs_d, recv_v, draft_value)


def feed_forward(rows_in, ln_gain, w_in, w_out):
    inner = w_out.shape[0]
    floats = rows_in.astype(jnp.float32)
    mean_value = jnp.mean(floats, axis=1, keepdims=True)
    centred = floats - mean_value
    variance = jnp.mean(centred * centred, axis=1, keepdims=True)
    normed = (centred * lax.rsqrt(variance + 1e-05) * ln_gain.astype(jnp.float32)[None, :]).astype(
        jnp.bfloat16
    )
    both = jnp.dot(normed, w_in, preferred_element_type=jnp.float32)
    middle = (jax.nn.gelu(both[:, :inner], approximate=False) * both[:, inner:]).astype(
        jnp.bfloat16
    )
    return jnp.dot(middle, w_out, preferred_element_type=jnp.float32).astype(jnp.bfloat16)


def local(
    hidden,
    draft_query,
    draft_key,
    draft_value,
    cache_keys,
    cache_values,
    page_target,
    page_slot,
    page_fill,
    tree_parent,
    tree_size,
    accepted_leaf,
    w_attn_out,
    ln_gain,
    w_in,
    w_out,
):
    devices = lax.axis_size("req")
    pages_here, page_len, width = cache_keys.shape
    per_target = max(2, -(-pages_here // devices))
    target = page_target[:, 0]
    onehot = (target[:, None] == jnp.arange(devices, dtype=jnp.int32)[None, :]).astype(jnp.int32)
    within = jnp.sum(jnp.cumsum(onehot, axis=0) * onehot, axis=1) - 1
    dest_slot = target * per_target + within
    slot_count = devices * per_target
    matches = dest_slot[None, :] == jnp.arange(slot_count, dtype=jnp.int32)[:, None]
    filled = jnp.any(matches, axis=1)
    source = jnp.sum(
        jnp.where(matches, jnp.arange(pages_here, dtype=jnp.int32)[None, :], 0), axis=1
    )
    send_meta = jnp.stack(
        [jnp.where(filled, page_fill[source], 0), page_slot[source]], axis=1
    ).reshape(devices, per_target * 2)
    recv_k = lax.all_to_all(
        cache_keys[source].reshape(devices, per_target, page_len, width), "req", 0, 0, tiled=True
    ).reshape(slot_count, page_len, width)
    recv_v = lax.all_to_all(
        cache_values[source].reshape(devices, per_target, page_len, width), "req", 0, 0, tiled=True
    ).reshape(slot_count, page_len, width)
    recv_meta = lax.all_to_all(send_meta, "req", 0, 0, tiled=True).reshape(slot_count, 2)
    recv_fill = recv_meta[:, 0]
    recv_owner = recv_meta[:, 1]
    requests, tree_width = tree_parent.shape
    rows = requests * tree_width
    ancestors = ancestor_closure(tree_parent)
    depth = (jnp.sum(ancestors, axis=2) - 1.0).astype(jnp.int32)
    request_ids = jnp.arange(requests, dtype=jnp.int32)
    cache_len = jnp.sum(
        jnp.where(recv_owner[None, :] == request_ids[:, None], recv_fill[None, :], 0), axis=1
    )
    positions = (cache_len[:, None] + depth).reshape(rows)
    query_rot = rotate_positions(draft_query, positions, HEADS)
    key_rot = rotate_positions(draft_key, positions, HEADS)
    key_owner = jnp.where(
        jnp.arange(page_len, dtype=jnp.int32)[None, :] < recv_fill[:, None], recv_owner[:, None], -1
    ).reshape(1, -1)
    tree_mask = (
        ancestors[:, :, None, :] * jnp.eye(requests, dtype=jnp.float32)[:, None, :, None]
    ).reshape(rows, rows)
    context = attend(query_rot, recv_k, recv_v, key_rot, draft_value, key_owner, tree_mask, tree_width)
    attended = (
        hidden.astype(jnp.float32)
        + jnp.dot(context, w_attn_out, preferred_element_type=jnp.float32)
    ).astype(jnp.bfloat16)
    alive_mask = (jnp.arange(tree_width, dtype=jnp.int32)[None, :] < tree_size[:, None]).reshape(
        rows
    )
    ffn_out = feed_forward(attended, ln_gain, w_in, w_out)
    layer_out = jnp.where(
        alive_mask[:, None], attended.astype(jnp.float32) + ffn_out.astype(jnp.float32), 0.0
    ).astype(jnp.bfloat16)
    leaf_index = jnp.minimum(accepted_leaf, tree_size - 1)
    leaf_onehot = (jnp.arange(tree_width, dtype=jnp.int32)[None, :] == leaf_index[:, None]).astype(
        jnp.float32
    )
    path = jnp.einsum("ri,rij->rj", leaf_onehot, ancestors, precision=lax.Precision.HIGHEST)
    select = (
        path[:, None, :]
        * (depth[:, None, :] == jnp.arange(tree_width, dtype=jnp.int32)[None, :, None]).astype(
            jnp.float32
        )
    ).astype(jnp.bfloat16)
    kept_keys = jnp.einsum(
        "rkj,rjd->rkd",
        select,
        key_rot.reshape(requests, tree_width, width),
        preferred_element_type=jnp.float32,
    )
    kept_values = jnp.einsum(
        "rkj,rjd->rkd",
        select,
        draft_value.reshape(requests, tree_width, width),
        preferred_element_type=jnp.float32,
    )
    return (
        layer_out,
        kept_keys.reshape(rows, width).astype(jnp.bfloat16),
        kept_values.reshape(rows, width).astype(jnp.bfloat16),
    )


def solution(mesh):
    placed = (
        P("req", None),
        P("req", None),
        P("req", None),
        P("req", None),
        P("req", None, None),
        P("req", None, None),
        P("req", None),
        P("req"),
        P("req"),
        P("req", None),
        P("req"),
        P("req"),
        P(),
        P(),
        P(),
        P(),
    )
    return jax.shard_map(
        local,
        mesh=mesh,
        in_specs=placed,
        out_specs=(P("req", None), P("req", None), P("req", None)),
        check_vma=False,
    )
```

```python
import functools

import jax
import jax.numpy as jnp
from jax import lax
from jax.experimental import pallas as pl
from jax.experimental.pallas import tpu as pltpu
from jax.sharding import PartitionSpec as P

HEADS = 16


def ancestor_closure(tree_parent):
    width = tree_parent.shape[1]
    ident = jnp.eye(width, dtype=jnp.float32)
    ancestors = (
        tree_parent[:, :, None] == jnp.arange(width, dtype=jnp.int32)[None, None, :]
    ).astype(jnp.float32) + ident
    for repeat in range((width - 1).bit_length()):
        ancestors = jnp.minimum(
            jnp.einsum("rij,rjk->rik", ancestors, ancestors, precision=lax.Precision.HIGHEST), 1.0
        )
    return ancestors


def rotate_positions(values, positions, heads):
    rows, width = values.shape
    head_size = width // heads
    half = head_size // 2
    inverse = jnp.power(160000.0, -(2.0 * jnp.arange(half, dtype=jnp.float32)) / head_size)
    angle = positions.astype(jnp.float32)[:, None] * inverse[None, :]
    cosine = jnp.cos(angle)[:, None, :]
    sine = jnp.sin(angle)[:, None, :]
    shaped = values.astype(jnp.float32).reshape(rows, heads, head_size)
    first = shaped[..., :half]
    second = shaped[..., half:]
    turned = jnp.concatenate(
        [first * cosine - second * sine, second * cosine + first * sine], axis=-1
    )
    return turned.reshape(rows, width).astype(jnp.bfloat16)


def _probs_kernel(q_ref, kc_ref, kd_ref, kown_ref, tmask_ref, pc_ref, pd_ref, *,
                  tree_width, head_size, scale):
    rows, lanes = q_ref.shape
    q = q_ref[...]
    kc = kc_ref[...].reshape(-1, lanes)
    kd = kd_ref[...]
    lane = lax.broadcasted_iota(jnp.int32, (1, lanes), 1)
    qown = lax.broadcasted_iota(jnp.int32, (rows, 1), 0) // tree_width
    cmask = qown == kown_ref[...]
    tmask = tmask_ref[...] > 0.5
    dims = (((1,), (1,)), ((), ()))
    for part in range(lanes // head_size):
        sel = (lane >= part * head_size) & (lane < (part + 1) * head_size)
        qh = jnp.where(sel, q, jnp.zeros((), q.dtype))
        sc = lax.dot_general(qh, kc, dims, preferred_element_type=jnp.float32) * scale
        sd = lax.dot_general(qh, kd, dims, preferred_element_type=jnp.float32) * scale
        sc = jnp.where(cmask, sc, -1e30)
        sd = jnp.where(tmask, sd, -1e30)
        top = jnp.maximum(jnp.max(sc, axis=1, keepdims=True), jnp.max(sd, axis=1, keepdims=True))
        pc = jnp.exp(sc - top)
        pd = jnp.exp(sd - top)
        inv = 1.0 / (jnp.sum(pc, axis=1, keepdims=True) + jnp.sum(pd, axis=1, keepdims=True))
        pc_ref[part] = (pc * inv).astype(pc_ref.dtype)
        pd_ref[part] = (pd * inv).astype(pd_ref.dtype)


def _context_kernel(pc_ref, pd_ref, vc_ref, vd_ref, o_ref, *, head_size):
    rows, lanes = o_ref.shape
    vc = vc_ref[...].reshape(-1, lanes)
    vd = vd_ref[...]
    lane = lax.broadcasted_iota(jnp.int32, (1, lanes), 1)
    result = None
    for part in range(lanes // head_size):
        ctx = jnp.dot(pc_ref[part], vc, preferred_element_type=jnp.float32)
        ctx = ctx + jnp.dot(pd_ref[part], vd, preferred_element_type=jnp.float32)
        if result is None:
            result = ctx
        else:
            sel = (lane >= part * head_size) & (lane < (part + 1) * head_size)
            result = jnp.where(sel, ctx, result)
    o_ref[...] = result.astype(o_ref.dtype)


def attend(query_rot, recv_k, recv_v, key_rot, draft_value, key_owner, tree_mask, tree_width):
    rows, width = query_rot.shape
    head_size = width // HEADS
    lanes = 128
    per = lanes // head_size
    groups = width // lanes
    slots, page_len, _ = recv_k.shape
    keys = slots * page_len
    params = pltpu.CompilerParams(vmem_limit_bytes=60 * 1024 * 1024)
    probs_c, probs_d = pl.pallas_call(
        functools.partial(
            _probs_kernel, tree_width=tree_width, head_size=head_size, scale=1.0 / head_size**0.5
        ),
        grid=(groups,),
        in_specs=[
            pl.BlockSpec((rows, lanes), lambda h: (0, h)),
            pl.BlockSpec((slots, page_len, lanes), lambda h: (0, 0, h)),
            pl.BlockSpec((rows, lanes), lambda h: (0, h)),
            pl.BlockSpec((1, keys), lambda h: (0, 0)),
            pl.BlockSpec((rows, rows), lambda h: (0, 0)),
        ],
        out_specs=[
            pl.BlockSpec((None, per, rows, keys), lambda h: (h, 0, 0, 0)),
            pl.BlockSpec((None, per, rows, rows), lambda h: (h, 0, 0, 0)),
        ],
        out_shape=[
            jax.ShapeDtypeStruct((groups, per, rows, keys), jnp.bfloat16),
            jax.ShapeDtypeStruct((groups, per, rows, rows), jnp.bfloat16),
        ],
        compiler_params=params,
    )(query_rot, recv_k, key_rot, key_owner, tree_mask)
    return pl.pallas_call(
        functools.partial(_context_kernel, head_size=head_size),
        grid=(groups,),
        in_specs=[
            pl.BlockSpec((None, per, rows, keys), lambda h: (h, 0, 0, 0)),
            pl.BlockSpec((None, per, rows, rows), lambda h: (h, 0, 0, 0)),
            pl.BlockSpec((slots, page_len, lanes), lambda h: (0, 0, h)),
            pl.BlockSpec((rows, lanes), lambda h: (0, h)),
        ],
        out_specs=pl.BlockSpec((rows, lanes), lambda h: (0, h)),
        out_shape=jax.ShapeDtypeStruct((rows, width), jnp.bfloat16),
        compiler_params=params,
    )(probs_c, probs_d, recv_v, draft_value)


def feed_forward(rows_in, ln_gain, w_in, w_out):
    inner = w_out.shape[0]
    floats = rows_in.astype(jnp.float32)
    mean_value = jnp.mean(floats, axis=1, keepdims=True)
    centred = floats - mean_value
    variance = jnp.mean(centred * centred, axis=1, keepdims=True)
    normed = (centred * lax.rsqrt(variance + 1e-05) * ln_gain.astype(jnp.float32)[None, :]).astype(
        jnp.bfloat16
    )
    both = jnp.dot(normed, w_in, preferred_element_type=jnp.float32)
    middle = (jax.nn.gelu(both[:, :inner], approximate=False) * both[:, inner:]).astype(
        jnp.bfloat16
    )
    return jnp.dot(middle, w_out, preferred_element_type=jnp.float32).astype(jnp.bfloat16)


def local(
    hidden,
    draft_query,
    draft_key,
    draft_value,
    cache_keys,
    cache_values,
    page_target,
    page_slot,
    page_fill,
    tree_parent,
    tree_size,
    accepted_leaf,
    w_attn_out,
    ln_gain,
    w_in,
    w_out,
):
    devices = lax.axis_size("req")
    pages_here, page_len, width = cache_keys.shape
    per_target = max(2, -(-pages_here // devices))
    target = page_target[:, 0]
    onehot = (target[:, None] == jnp.arange(devices, dtype=jnp.int32)[None, :]).astype(jnp.int32)
    within = jnp.sum(jnp.cumsum(onehot, axis=0) * onehot, axis=1) - 1
    dest_slot = target * per_target + within
    slot_count = devices * per_target
    matches = dest_slot[None, :] == jnp.arange(slot_count, dtype=jnp.int32)[:, None]
    filled = jnp.any(matches, axis=1)
    source = jnp.sum(
        jnp.where(matches, jnp.arange(pages_here, dtype=jnp.int32)[None, :], 0), axis=1
    )
    recv_k = lax.all_to_all(
        cache_keys[source].reshape(devices, per_target, page_len, width), "req", 0, 0, tiled=True
    ).reshape(slot_count, page_len, width)
    recv_v = lax.all_to_all(
        cache_values[source].reshape(devices, per_target, page_len, width), "req", 0, 0, tiled=True
    ).reshape(slot_count, page_len, width)
    table = lax.all_gather(
        jnp.stack([target, page_slot, page_fill], axis=0), "req", axis=0, tiled=False
    )
    mine = table[:, 0, :] == lax.axis_index("req")
    rank = jnp.cumsum(mine.astype(jnp.int32), axis=1) - 1
    hit = mine[:, None, :] & (rank[:, None, :] == jnp.arange(per_target, dtype=jnp.int32)[None, :, None])
    recv_fill = jnp.sum(jnp.where(hit, table[:, None, 2, :], 0), axis=2).reshape(slot_count)
    recv_owner = jnp.sum(jnp.where(hit, table[:, None, 1, :], 0), axis=2).reshape(slot_count)
    requests, tree_width = tree_parent.shape
    rows = requests * tree_width
    ancestors = ancestor_closure(tree_parent)
    depth = (jnp.sum(ancestors, axis=2) - 1.0).astype(jnp.int32)
    request_ids = jnp.arange(requests, dtype=jnp.int32)
    cache_len = jnp.sum(
        jnp.where(recv_owner[None, :] == request_ids[:, None], recv_fill[None, :], 0), axis=1
    )
    positions = (cache_len[:, None] + depth).reshape(rows)
    query_rot = rotate_positions(draft_query, positions, HEADS)
    key_rot = rotate_positions(draft_key, positions, HEADS)
    key_owner = jnp.where(
        jnp.arange(page_len, dtype=jnp.int32)[None, :] < recv_fill[:, None], recv_owner[:, None], -1
    ).reshape(1, -1)
    tree_mask = (
        ancestors[:, :, None, :] * jnp.eye(requests, dtype=jnp.float32)[:, None, :, None]
    ).reshape(rows, rows)
    context = attend(query_rot, recv_k, recv_v, key_rot, draft_value, key_owner, tree_mask, tree_width)
    attended = (
        hidden.astype(jnp.float32)
        + jnp.dot(context, w_attn_out, preferred_element_type=jnp.float32)
    ).astype(jnp.bfloat16)
    alive_mask = (jnp.arange(tree_width, dtype=jnp.int32)[None, :] < tree_size[:, None]).reshape(
        rows
    )
    ffn_out = feed_forward(attended, ln_gain, w_in, w_out)
    layer_out = jnp.where(
        alive_mask[:, None], attended.astype(jnp.float32) + ffn_out.astype(jnp.float32), 0.0
    ).astype(jnp.bfloat16)
    leaf_index = jnp.minimum(accepted_leaf, tree_size - 1)
    leaf_onehot = (jnp.arange(tree_width, dtype=jnp.int32)[None, :] == leaf_index[:, None]).astype(
        jnp.float32
    )
    path = jnp.einsum("ri,rij->rj", leaf_onehot, ancestors, precision=lax.Precision.HIGHEST)
    select = (
        path[:, None, :]
        * (depth[:, None, :] == jnp.arange(tree_width, dtype=jnp.int32)[None, :, None]).astype(
            jnp.float32
        )
    ).astype(jnp.bfloat16)
    kept_keys = jnp.einsum(
        "rkj,rjd->rkd",
        select,
        key_rot.reshape(requests, tree_width, width),
        preferred_element_type=jnp.float32,
    )
    kept_values = jnp.einsum(
        "rkj,rjd->rkd",
        select,
        draft_value.reshape(requests, tree_width, width),
        preferred_element_type=jnp.float32,
    )
    return (
        layer_out,
        kept_keys.reshape(rows, width).astype(jnp.bfloat16),
        kept_values.reshape(rows, width).astype(jnp.bfloat16),
    )


def solution(mesh):
    placed = (
        P("req", None),
        P("req", None),
        P("req", None),
        P("req", None),
        P("req", None, None),
        P("req", None, None),
        P("req", None),
        P("req"),
        P("req"),
        P("req", None),
        P("req"),
        P("req"),
        P(),
        P(),
        P(),
        P(),
    )
    return jax.shard_map(
        local,
        mesh=mesh,
        in_specs=placed,
        out_specs=(P("req", None), P("req", None), P("req", None)),
        check_vma=False,
    )
```

```python
import functools

import jax
import jax.numpy as jnp
from jax import lax
from jax.experimental import pallas as pl
from jax.experimental.pallas import tpu as pltpu
from jax.sharding import PartitionSpec as P

HEADS = 16


def ancestor_closure(tree_parent):
    width = tree_parent.shape[1]
    ident = jnp.eye(width, dtype=jnp.float32)
    ancestors = (
        tree_parent[:, :, None] == jnp.arange(width, dtype=jnp.int32)[None, None, :]
    ).astype(jnp.float32) + ident
    for repeat in range((width - 1).bit_length()):
        ancestors = jnp.minimum(
            jnp.einsum("rij,rjk->rik", ancestors, ancestors, precision=lax.Precision.HIGHEST), 1.0
        )
    return ancestors


def rotate_positions(values, positions, heads):
    rows, width = values.shape
    head_size = width // heads
    half = head_size // 2
    inverse = jnp.power(160000.0, -(2.0 * jnp.arange(half, dtype=jnp.float32)) / head_size)
    angle = positions.astype(jnp.float32)[:, None] * inverse[None, :]
    cosine = jnp.cos(angle)[:, None, :]
    sine = jnp.sin(angle)[:, None, :]
    shaped = values.astype(jnp.float32).reshape(rows, heads, head_size)
    first = shaped[..., :half]
    second = shaped[..., half:]
    turned = jnp.concatenate(
        [first * cosine - second * sine, second * cosine + first * sine], axis=-1
    )
    return turned.reshape(rows, width).astype(jnp.bfloat16)


def _probs_kernel(q_ref, kc_ref, kd_ref, kown_ref, tmask_ref, pc_ref, pd_ref, *,
                  tree_width, head_size, scale):
    rows, lanes = q_ref.shape
    q = q_ref[...]
    kc = kc_ref[...].reshape(-1, lanes)
    kd = kd_ref[...]
    lane = lax.broadcasted_iota(jnp.int32, (1, lanes), 1)
    qown = lax.broadcasted_iota(jnp.int32, (rows, 1), 0) // tree_width
    cmask = qown == kown_ref[...]
    tmask = tmask_ref[...] > 0.5
    dims = (((1,), (1,)), ((), ()))
    for part in range(lanes // head_size):
        sel = (lane >= part * head_size) & (lane < (part + 1) * head_size)
        qh = jnp.where(sel, q, jnp.zeros((), q.dtype))
        sc = lax.dot_general(qh, kc, dims, preferred_element_type=jnp.float32) * scale
        sd = lax.dot_general(qh, kd, dims, preferred_element_type=jnp.float32) * scale
        sc = jnp.where(cmask, sc, -1e30)
        sd = jnp.where(tmask, sd, -1e30)
        top = jnp.maximum(jnp.max(sc, axis=1, keepdims=True), jnp.max(sd, axis=1, keepdims=True))
        pc = jnp.exp(sc - top)
        pd = jnp.exp(sd - top)
        inv = 1.0 / (jnp.sum(pc, axis=1, keepdims=True) + jnp.sum(pd, axis=1, keepdims=True))
        pc_ref[part] = (pc * inv).astype(pc_ref.dtype)
        pd_ref[part] = (pd * inv).astype(pd_ref.dtype)


def _context_kernel(pc_ref, pd_ref, vc_ref, vd_ref, o_ref, *, head_size):
    rows, lanes = o_ref.shape
    vc = vc_ref[...].reshape(-1, lanes)
    vd = vd_ref[...]
    lane = lax.broadcasted_iota(jnp.int32, (1, lanes), 1)
    result = None
    for part in range(lanes // head_size):
        ctx = jnp.dot(pc_ref[part], vc, preferred_element_type=jnp.float32)
        ctx = ctx + jnp.dot(pd_ref[part], vd, preferred_element_type=jnp.float32)
        if result is None:
            result = ctx
        else:
            sel = (lane >= part * head_size) & (lane < (part + 1) * head_size)
            result = jnp.where(sel, ctx, result)
    o_ref[...] = result.astype(o_ref.dtype)


def attend(query_rot, recv_k, recv_v, key_rot, draft_value, key_owner, tree_mask, tree_width):
    rows, width = query_rot.shape
    head_size = width // HEADS
    lanes = 128
    per = lanes // head_size
    groups = width // lanes
    slots, page_len, _ = recv_v.shape
    keys = slots * page_len
    sources = recv_k.shape[0]
    block_rows = keys // sources
    params = pltpu.CompilerParams(vmem_limit_bytes=60 * 1024 * 1024)
    probs_c, probs_d = pl.pallas_call(
        functools.partial(
            _probs_kernel, tree_width=tree_width, head_size=head_size, scale=1.0 / head_size**0.5
        ),
        grid=(groups,),
        in_specs=[
            pl.BlockSpec((rows, lanes), lambda h: (0, h)),
            pl.BlockSpec((sources, block_rows, lanes), lambda h: (0, 0, h)),
            pl.BlockSpec((rows, lanes), lambda h: (0, h)),
            pl.BlockSpec((1, keys), lambda h: (0, 0)),
            pl.BlockSpec((rows, rows), lambda h: (0, 0)),
        ],
        out_specs=[
            pl.BlockSpec((None, per, rows, keys), lambda h: (h, 0, 0, 0)),
            pl.BlockSpec((None, per, rows, rows), lambda h: (h, 0, 0, 0)),
        ],
        out_shape=[
            jax.ShapeDtypeStruct((groups, per, rows, keys), jnp.bfloat16),
            jax.ShapeDtypeStruct((groups, per, rows, rows), jnp.bfloat16),
        ],
        compiler_params=params,
    )(query_rot, recv_k, key_rot, key_owner, tree_mask)
    return pl.pallas_call(
        functools.partial(_context_kernel, head_size=head_size),
        grid=(groups,),
        in_specs=[
            pl.BlockSpec((None, per, rows, keys), lambda h: (h, 0, 0, 0)),
            pl.BlockSpec((None, per, rows, rows), lambda h: (h, 0, 0, 0)),
            pl.BlockSpec((slots, page_len, lanes), lambda h: (0, 0, h)),
            pl.BlockSpec((rows, lanes), lambda h: (0, h)),
        ],
        out_specs=pl.BlockSpec((rows, lanes), lambda h: (0, h)),
        out_shape=jax.ShapeDtypeStruct((rows, width), jnp.bfloat16),
        compiler_params=params,
    )(probs_c, probs_d, recv_v, draft_value)


def feed_forward(rows_in, ln_gain, w_in, w_out):
    inner = w_out.shape[0]
    floats = rows_in.astype(jnp.float32)
    mean_value = jnp.mean(floats, axis=1, keepdims=True)
    centred = floats - mean_value
    variance = jnp.mean(centred * centred, axis=1, keepdims=True)
    normed = (centred * lax.rsqrt(variance + 1e-05) * ln_gain.astype(jnp.float32)[None, :]).astype(
        jnp.bfloat16
    )
    both = jnp.dot(normed, w_in, preferred_element_type=jnp.float32)
    middle = (jax.nn.gelu(both[:, :inner], approximate=False) * both[:, inner:]).astype(
        jnp.bfloat16
    )
    return jnp.dot(middle, w_out, preferred_element_type=jnp.float32).astype(jnp.bfloat16)


def local(
    hidden,
    draft_query,
    draft_key,
    draft_value,
    cache_keys,
    cache_values,
    page_target,
    page_slot,
    page_fill,
    tree_parent,
    tree_size,
    accepted_leaf,
    w_attn_out,
    ln_gain,
    w_in,
    w_out,
):
    devices = lax.axis_size("req")
    pages_here, page_len, width = cache_keys.shape
    per_target = max(2, -(-pages_here // devices))
    target = page_target[:, 0]
    onehot = (target[:, None] == jnp.arange(devices, dtype=jnp.int32)[None, :]).astype(jnp.int32)
    within = jnp.sum(jnp.cumsum(onehot, axis=0) * onehot, axis=1) - 1
    dest_slot = target * per_target + within
    slot_count = devices * per_target
    matches = dest_slot[None, :] == jnp.arange(slot_count, dtype=jnp.int32)[:, None]
    filled = jnp.any(matches, axis=1)
    source = jnp.sum(
        jnp.where(matches, jnp.arange(pages_here, dtype=jnp.int32)[None, :], 0), axis=1
    )
    send_fill = jnp.sum(jnp.where(matches, page_fill[None, :], 0), axis=1)
    send_owner = jnp.sum(jnp.where(matches, page_slot[None, :], 0), axis=1)
    meta_row = jnp.concatenate(
        [
            jnp.stack([send_fill, send_owner], axis=1).reshape(devices, 2 * per_target),
            jnp.zeros((devices, width - 2 * per_target), jnp.int32),
        ],
        axis=1,
    ).astype(jnp.bfloat16)
    table = jnp.concatenate([cache_keys.reshape(pages_here * page_len, width), meta_row], axis=0)
    row_ids = jnp.concatenate(
        [
            (source[:, None] * page_len + jnp.arange(page_len, dtype=jnp.int32)[None, :]).reshape(
                devices, per_target * page_len
            ),
            pages_here * page_len + jnp.arange(devices, dtype=jnp.int32)[:, None],
        ],
        axis=1,
    )
    send_k = table[row_ids]
    recv_k = lax.all_to_all(send_k, "req", 0, 0, tiled=True)
    recv_v = lax.all_to_all(
        cache_values[source].reshape(devices, per_target, page_len, width), "req", 0, 0, tiled=True
    ).reshape(slot_count, page_len, width)
    recv_meta = recv_k[:, per_target * page_len, : 2 * per_target].astype(jnp.int32)
    recv_meta = recv_meta.reshape(slot_count, 2)
    recv_fill = recv_meta[:, 0]
    recv_owner = recv_meta[:, 1]
    requests, tree_width = tree_parent.shape
    rows = requests * tree_width
    ancestors = ancestor_closure(tree_parent)
    depth = (jnp.sum(ancestors, axis=2) - 1.0).astype(jnp.int32)
    request_ids = jnp.arange(requests, dtype=jnp.int32)
    cache_len = jnp.sum(
        jnp.where(recv_owner[None, :] == request_ids[:, None], recv_fill[None, :], 0), axis=1
    )
    positions = (cache_len[:, None] + depth).reshape(rows)
    query_rot = rotate_positions(draft_query, positions, HEADS)
    key_rot = rotate_positions(draft_key, positions, HEADS)
    key_owner = jnp.where(
        jnp.arange(page_len, dtype=jnp.int32)[None, :] < recv_fill[:, None], recv_owner[:, None], -1
    ).reshape(1, -1)
    tree_mask = (
        ancestors[:, :, None, :] * jnp.eye(requests, dtype=jnp.float32)[:, None, :, None]
    ).reshape(rows, rows)
    context = attend(query_rot, recv_k, recv_v, key_rot, draft_value, key_owner, tree_mask, tree_width)
    attended = (
        hidden.astype(jnp.float32)
        + jnp.dot(context, w_attn_out, preferred_element_type=jnp.float32)
    ).astype(jnp.bfloat16)
    alive_mask = (jnp.arange(tree_width, dtype=jnp.int32)[None, :] < tree_size[:, None]).reshape(
        rows
    )
    ffn_out = feed_forward(attended, ln_gain, w_in, w_out)
    layer_out = jnp.where(
        alive_mask[:, None], attended.astype(jnp.float32) + ffn_out.astype(jnp.float32), 0.0
    ).astype(jnp.bfloat16)
    leaf_index = jnp.minimum(accepted_leaf, tree_size - 1)
    leaf_onehot = (jnp.arange(tree_width, dtype=jnp.int32)[None, :] == leaf_index[:, None]).astype(
        jnp.float32
    )
    path = jnp.einsum("ri,rij->rj", leaf_onehot, ancestors, precision=lax.Precision.HIGHEST)
    select = (
        path[:, None, :]
        * (depth[:, None, :] == jnp.arange(tree_width, dtype=jnp.int32)[None, :, None]).astype(
            jnp.float32
        )
    ).astype(jnp.bfloat16)
    kept_keys = jnp.einsum(
        "rkj,rjd->rkd",
        select,
        key_rot.reshape(requests, tree_width, width),
        preferred_element_type=jnp.float32,
    )
    kept_values = jnp.einsum(
        "rkj,rjd->rkd",
        select,
        draft_value.reshape(requests, tree_width, width),
        preferred_element_type=jnp.float32,
    )
    return (
        layer_out,
        kept_keys.reshape(rows, width).astype(jnp.bfloat16),
        kept_values.reshape(rows, width).astype(jnp.bfloat16),
    )


def solution(mesh):
    placed = (
        P("req", None),
        P("req", None),
        P("req", None),
        P("req", None),
        P("req", None, None),
        P("req", None, None),
        P("req", None),
        P("req"),
        P("req"),
        P("req", None),
        P("req"),
        P("req"),
        P(),
        P(),
        P(),
        P(),
    )
    return jax.shard_map(
        local,
        mesh=mesh,
        in_specs=placed,
        out_specs=(P("req", None), P("req", None), P("req", None)),
        check_vma=False,
    )
```

```python
import functools

import jax
import jax.numpy as jnp
from jax import lax
from jax.experimental import pallas as pl
from jax.experimental.pallas import tpu as pltpu
from jax.sharding import PartitionSpec as P

HEADS = 16


def ancestor_closure(tree_parent):
    width = tree_parent.shape[1]
    ident = jnp.eye(width, dtype=jnp.float32)
    ancestors = (
        tree_parent[:, :, None] == jnp.arange(width, dtype=jnp.int32)[None, None, :]
    ).astype(jnp.float32) + ident
    for repeat in range((width - 1).bit_length()):
        ancestors = jnp.minimum(
            jnp.einsum("rij,rjk->rik", ancestors, ancestors, precision=lax.Precision.HIGHEST), 1.0
        )
    return ancestors


def rotate_positions(values, positions, heads):
    rows, width = values.shape
    head_size = width // heads
    half = head_size // 2
    inverse = jnp.power(160000.0, -(2.0 * jnp.arange(half, dtype=jnp.float32)) / head_size)
    angle = positions.astype(jnp.float32)[:, None] * inverse[None, :]
    cosine = jnp.cos(angle)[:, None, :]
    sine = jnp.sin(angle)[:, None, :]
    shaped = values.astype(jnp.float32).reshape(rows, heads, head_size)
    first = shaped[..., :half]
    second = shaped[..., half:]
    turned = jnp.concatenate(
        [first * cosine - second * sine, second * cosine + first * sine], axis=-1
    )
    return turned.reshape(rows, width).astype(jnp.bfloat16)


def _probs_kernel(q_ref, kc_ref, kd_ref, kown_ref, tmask_ref, pc_ref, pd_ref, *,
                  tree_width, head_size, scale):
    rows, lanes = q_ref.shape
    q = q_ref[...]
    kc = kc_ref[...].reshape(-1, lanes)
    kd = kd_ref[...]
    lane = lax.broadcasted_iota(jnp.int32, (1, lanes), 1)
    qown = lax.broadcasted_iota(jnp.int32, (rows, 1), 0) // tree_width
    cmask = qown == kown_ref[...]
    tmask = tmask_ref[...] > 0.5
    dims = (((1,), (1,)), ((), ()))
    for part in range(lanes // head_size):
        sel = (lane >= part * head_size) & (lane < (part + 1) * head_size)
        qh = jnp.where(sel, q, jnp.zeros((), q.dtype))
        sc = lax.dot_general(qh, kc, dims, preferred_element_type=jnp.float32) * scale
        sd = lax.dot_general(qh, kd, dims, preferred_element_type=jnp.float32) * scale
        sc = jnp.where(cmask, sc, -1e30)
        sd = jnp.where(tmask, sd, -1e30)
        top = jnp.maximum(jnp.max(sc, axis=1, keepdims=True), jnp.max(sd, axis=1, keepdims=True))
        pc = jnp.exp(sc - top)
        pd = jnp.exp(sd - top)
        inv = 1.0 / (jnp.sum(pc, axis=1, keepdims=True) + jnp.sum(pd, axis=1, keepdims=True))
        pc_ref[part] = (pc * inv).astype(pc_ref.dtype)
        pd_ref[part] = (pd * inv).astype(pd_ref.dtype)


def _context_kernel(pc_ref, pd_ref, vc_ref, vd_ref, o_ref, *, head_size):
    rows, lanes = o_ref.shape
    vc = vc_ref[...].reshape(-1, lanes)
    vd = vd_ref[...]
    lane = lax.broadcasted_iota(jnp.int32, (1, lanes), 1)
    result = None
    for part in range(lanes // head_size):
        ctx = jnp.dot(pc_ref[part], vc, preferred_element_type=jnp.float32)
        ctx = ctx + jnp.dot(pd_ref[part], vd, preferred_element_type=jnp.float32)
        if result is None:
            result = ctx
        else:
            sel = (lane >= part * head_size) & (lane < (part + 1) * head_size)
            result = jnp.where(sel, ctx, result)
    o_ref[...] = result.astype(o_ref.dtype)


def attend(query_rot, recv_k, recv_v, key_rot, draft_value, key_owner, tree_mask, tree_width):
    rows, width = query_rot.shape
    head_size = width // HEADS
    lanes = 128
    per = lanes // head_size
    groups = width // lanes
    slots, page_len, _ = recv_k.shape
    keys = slots * page_len
    params = pltpu.CompilerParams(vmem_limit_bytes=60 * 1024 * 1024)
    probs_c, probs_d = pl.pallas_call(
        functools.partial(
            _probs_kernel, tree_width=tree_width, head_size=head_size, scale=1.0 / head_size**0.5
        ),
        grid=(groups,),
        in_specs=[
            pl.BlockSpec((rows, lanes), lambda h: (0, h)),
            pl.BlockSpec((slots, page_len, lanes), lambda h: (0, 0, h)),
            pl.BlockSpec((rows, lanes), lambda h: (0, h)),
            pl.BlockSpec((1, keys), lambda h: (0, 0)),
            pl.BlockSpec((rows, rows), lambda h: (0, 0)),
        ],
        out_specs=[
            pl.BlockSpec((None, per, rows, keys), lambda h: (h, 0, 0, 0)),
            pl.BlockSpec((None, per, rows, rows), lambda h: (h, 0, 0, 0)),
        ],
        out_shape=[
            jax.ShapeDtypeStruct((groups, per, rows, keys), jnp.bfloat16),
            jax.ShapeDtypeStruct((groups, per, rows, rows), jnp.bfloat16),
        ],
        compiler_params=params,
    )(query_rot, recv_k, key_rot, key_owner, tree_mask)
    return pl.pallas_call(
        functools.partial(_context_kernel, head_size=head_size),
        grid=(groups,),
        in_specs=[
            pl.BlockSpec((None, per, rows, keys), lambda h: (h, 0, 0, 0)),
            pl.BlockSpec((None, per, rows, rows), lambda h: (h, 0, 0, 0)),
            pl.BlockSpec((slots, page_len, lanes), lambda h: (0, 0, h)),
            pl.BlockSpec((rows, lanes), lambda h: (0, h)),
        ],
        out_specs=pl.BlockSpec((rows, lanes), lambda h: (0, h)),
        out_shape=jax.ShapeDtypeStruct((rows, width), jnp.bfloat16),
        compiler_params=params,
    )(probs_c, probs_d, recv_v, draft_value)


def feed_forward(rows_in, ln_gain, w_in, w_out):
    inner = w_out.shape[0]
    floats = rows_in.astype(jnp.float32)
    mean_value = jnp.mean(floats, axis=1, keepdims=True)
    centred = floats - mean_value
    variance = jnp.mean(centred * centred, axis=1, keepdims=True)
    normed = (centred * lax.rsqrt(variance + 1e-05) * ln_gain.astype(jnp.float32)[None, :]).astype(
        jnp.bfloat16
    )
    both = jnp.dot(normed, w_in, preferred_element_type=jnp.float32)
    middle = (jax.nn.gelu(both[:, :inner], approximate=False) * both[:, inner:]).astype(
        jnp.bfloat16
    )
    return jnp.dot(middle, w_out, preferred_element_type=jnp.float32).astype(jnp.bfloat16)


def local(
    hidden,
    draft_query,
    draft_key,
    draft_value,
    cache_keys,
    cache_values,
    page_target,
    page_slot,
    page_fill,
    tree_parent,
    tree_size,
    accepted_leaf,
    w_attn_out,
    ln_gain,
    w_in,
    w_out,
):
    devices = lax.axis_size("req")
    pages_here, page_len, width = cache_keys.shape
    per_target = max(2, -(-pages_here // devices))
    target = page_target[:, 0]
    onehot = (target[:, None] == jnp.arange(devices, dtype=jnp.int32)[None, :]).astype(jnp.int32)
    within = jnp.sum(jnp.cumsum(onehot, axis=0) * onehot, axis=1) - 1
    dest_slot = target * per_target + within
    slot_count = devices * per_target
    matches = dest_slot[None, :] == jnp.arange(slot_count, dtype=jnp.int32)[:, None]
    filled = jnp.any(matches, axis=1)
    source = jnp.sum(
        jnp.where(matches, jnp.arange(pages_here, dtype=jnp.int32)[None, :], 0), axis=1
    )
    send_fill = jnp.sum(jnp.where(matches, page_fill[None, :], 0), axis=1)
    send_owner = jnp.sum(jnp.where(matches, page_slot[None, :], 0), axis=1)
    send_meta = jnp.stack([send_fill, send_owner], axis=1).reshape(devices, 1, per_target * 2)
    spread = jnp.zeros((devices, devices, per_target * 2), jnp.int32)
    spread = lax.dynamic_update_slice_in_dim(spread, send_meta, lax.axis_index("req"), axis=1)
    recv_meta = lax.psum_scatter(spread, "req", scatter_dimension=0, tiled=True)
    recv_meta = recv_meta.reshape(slot_count, 2)
    recv_k = lax.all_to_all(
        cache_keys[source].reshape(devices, per_target, page_len, width), "req", 0, 0, tiled=True
    ).reshape(slot_count, page_len, width)
    recv_v = lax.all_to_all(
        cache_values[source].reshape(devices, per_target, page_len, width), "req", 0, 0, tiled=True
    ).reshape(slot_count, page_len, width)
    recv_fill = recv_meta[:, 0]
    recv_owner = recv_meta[:, 1]
    requests, tree_width = tree_parent.shape
    rows = requests * tree_width
    ancestors = ancestor_closure(tree_parent)
    depth = (jnp.sum(ancestors, axis=2) - 1.0).astype(jnp.int32)
    request_ids = jnp.arange(requests, dtype=jnp.int32)
    cache_len = jnp.sum(
        jnp.where(recv_owner[None, :] == request_ids[:, None], recv_fill[None, :], 0), axis=1
    )
    positions = (cache_len[:, None] + depth).reshape(rows)
    query_rot = rotate_positions(draft_query, positions, HEADS)
    key_rot = rotate_positions(draft_key, positions, HEADS)
    key_owner = jnp.where(
        jnp.arange(page_len, dtype=jnp.int32)[None, :] < recv_fill[:, None], recv_owner[:, None], -1
    ).reshape(1, -1)
    tree_mask = (
        ancestors[:, :, None, :] * jnp.eye(requests, dtype=jnp.float32)[:, None, :, None]
    ).reshape(rows, rows)
    context = attend(query_rot, recv_k, recv_v, key_rot, draft_value, key_owner, tree_mask, tree_width)
    attended = (
        hidden.astype(jnp.float32)
        + jnp.dot(context, w_attn_out, preferred_element_type=jnp.float32)
    ).astype(jnp.bfloat16)
    alive_mask = (jnp.arange(tree_width, dtype=jnp.int32)[None, :] < tree_size[:, None]).reshape(
        rows
    )
    ffn_out = feed_forward(attended, ln_gain, w_in, w_out)
    layer_out = jnp.where(
        alive_mask[:, None], attended.astype(jnp.float32) + ffn_out.astype(jnp.float32), 0.0
    ).astype(jnp.bfloat16)
    leaf_index = jnp.minimum(accepted_leaf, tree_size - 1)
    leaf_onehot = (jnp.arange(tree_width, dtype=jnp.int32)[None, :] == leaf_index[:, None]).astype(
        jnp.float32
    )
    path = jnp.einsum("ri,rij->rj", leaf_onehot, ancestors, precision=lax.Precision.HIGHEST)
    select = (
        path[:, None, :]
        * (depth[:, None, :] == jnp.arange(tree_width, dtype=jnp.int32)[None, :, None]).astype(
            jnp.float32
        )
    ).astype(jnp.bfloat16)
    kept_keys = jnp.einsum(
        "rkj,rjd->rkd",
        select,
        key_rot.reshape(requests, tree_width, width),
        preferred_element_type=jnp.float32,
    )
    kept_values = jnp.einsum(
        "rkj,rjd->rkd",
        select,
        draft_value.reshape(requests, tree_width, width),
        preferred_element_type=jnp.float32,
    )
    return (
        layer_out,
        kept_keys.reshape(rows, width).astype(jnp.bfloat16),
        kept_values.reshape(rows, width).astype(jnp.bfloat16),
    )


def solution(mesh):
    placed = (
        P("req", None),
        P("req", None),
        P("req", None),
        P("req", None),
        P("req", None, None),
        P("req", None, None),
        P("req", None),
        P("req"),
        P("req"),
        P("req", None),
        P("req"),
        P("req"),
        P(),
        P(),
        P(),
        P(),
    )
    return jax.shard_map(
        local,
        mesh=mesh,
        in_specs=placed,
        out_specs=(P("req", None), P("req", None), P("req", None)),
        check_vma=False,
    )
```

```python
import functools

import jax
import jax.numpy as jnp
from jax import lax
from jax.experimental import pallas as pl
from jax.experimental.pallas import tpu as pltpu
from jax.sharding import PartitionSpec as P

HEADS = 16


def ancestor_closure(tree_parent):
    width = tree_parent.shape[1]
    ident = jnp.eye(width, dtype=jnp.float32)
    ancestors = (
        tree_parent[:, :, None] == jnp.arange(width, dtype=jnp.int32)[None, None, :]
    ).astype(jnp.float32) + ident
    for repeat in range((width - 1).bit_length()):
        ancestors = jnp.minimum(
            jnp.einsum("rij,rjk->rik", ancestors, ancestors, precision=lax.Precision.HIGHEST), 1.0
        )
    return ancestors


def rotate_positions(values, positions, heads):
    rows, width = values.shape
    head_size = width // heads
    half = head_size // 2
    inverse = jnp.power(160000.0, -(2.0 * jnp.arange(half, dtype=jnp.float32)) / head_size)
    angle = positions.astype(jnp.float32)[:, None] * inverse[None, :]
    cosine = jnp.cos(angle)[:, None, :]
    sine = jnp.sin(angle)[:, None, :]
    shaped = values.astype(jnp.float32).reshape(rows, heads, head_size)
    first = shaped[..., :half]
    second = shaped[..., half:]
    turned = jnp.concatenate(
        [first * cosine - second * sine, second * cosine + first * sine], axis=-1
    )
    return turned.reshape(rows, width).astype(jnp.bfloat16)


def _probs_kernel(q_ref, kc_ref, kd_ref, kown_ref, tmask_ref, pc_ref, pd_ref, *,
                  tree_width, head_size, scale):
    rows, lanes = q_ref.shape
    q = q_ref[...]
    kc = kc_ref[...].reshape(-1, lanes)
    kd = kd_ref[...]
    lane = lax.broadcasted_iota(jnp.int32, (1, lanes), 1)
    qown = lax.broadcasted_iota(jnp.int32, (rows, 1), 0) // tree_width
    cmask = qown == kown_ref[...]
    tmask = tmask_ref[...] > 0.5
    dims = (((1,), (1,)), ((), ()))
    for part in range(lanes // head_size):
        sel = (lane >= part * head_size) & (lane < (part + 1) * head_size)
        qh = jnp.where(sel, q, jnp.zeros((), q.dtype))
        sc = lax.dot_general(qh, kc, dims, preferred_element_type=jnp.float32) * scale
        sd = lax.dot_general(qh, kd, dims, preferred_element_type=jnp.float32) * scale
        sc = jnp.where(cmask, sc, -1e30)
        sd = jnp.where(tmask, sd, -1e30)
        top = jnp.maximum(jnp.max(sc, axis=1, keepdims=True), jnp.max(sd, axis=1, keepdims=True))
        pc = jnp.exp(sc - top)
        pd = jnp.exp(sd - top)
        inv = 1.0 / (jnp.sum(pc, axis=1, keepdims=True) + jnp.sum(pd, axis=1, keepdims=True))
        pc_ref[part] = (pc * inv).astype(pc_ref.dtype)
        pd_ref[part] = (pd * inv).astype(pd_ref.dtype)


def _context_kernel(pc_ref, pd_ref, vc_ref, vd_ref, o_ref, *, head_size):
    rows, lanes = o_ref.shape
    start = pl.multiple_of(pl.program_id(0) * lanes, lanes)
    vc = vc_ref[:, :, pl.ds(start, lanes)].reshape(-1, lanes)
    vd = vd_ref[...]
    lane = lax.broadcasted_iota(jnp.int32, (1, lanes), 1)
    result = None
    for part in range(lanes // head_size):
        ctx = jnp.dot(pc_ref[part], vc, preferred_element_type=jnp.float32)
        ctx = ctx + jnp.dot(pd_ref[part], vd, preferred_element_type=jnp.float32)
        if result is None:
            result = ctx
        else:
            sel = (lane >= part * head_size) & (lane < (part + 1) * head_size)
            result = jnp.where(sel, ctx, result)
    o_ref[...] = result.astype(o_ref.dtype)


def attend(query_rot, recv_k, recv_v, key_rot, draft_value, key_owner, tree_mask, tree_width):
    rows, width = query_rot.shape
    head_size = width // HEADS
    lanes = 128
    per = lanes // head_size
    groups = width // lanes
    slots, page_len, _ = recv_k.shape
    keys = slots * page_len
    params = pltpu.CompilerParams(vmem_limit_bytes=60 * 1024 * 1024)
    probs_c, probs_d = pl.pallas_call(
        functools.partial(
            _probs_kernel, tree_width=tree_width, head_size=head_size, scale=1.0 / head_size**0.5
        ),
        grid=(groups,),
        in_specs=[
            pl.BlockSpec((rows, lanes), lambda h: (0, h)),
            pl.BlockSpec((slots, page_len, lanes), lambda h: (0, 0, h)),
            pl.BlockSpec((rows, lanes), lambda h: (0, h)),
            pl.BlockSpec((1, keys), lambda h: (0, 0)),
            pl.BlockSpec((rows, rows), lambda h: (0, 0)),
        ],
        out_specs=[
            pl.BlockSpec((None, per, rows, keys), lambda h: (h, 0, 0, 0)),
            pl.BlockSpec((None, per, rows, rows), lambda h: (h, 0, 0, 0)),
        ],
        out_shape=[
            jax.ShapeDtypeStruct((groups, per, rows, keys), jnp.bfloat16),
            jax.ShapeDtypeStruct((groups, per, rows, rows), jnp.bfloat16),
        ],
        compiler_params=params,
    )(query_rot, recv_k, key_rot, key_owner, tree_mask)
    return pl.pallas_call(
        functools.partial(_context_kernel, head_size=head_size),
        grid=(groups,),
        in_specs=[
            pl.BlockSpec((None, per, rows, keys), lambda h: (h, 0, 0, 0)),
            pl.BlockSpec((None, per, rows, rows), lambda h: (h, 0, 0, 0)),
            pl.BlockSpec((slots, page_len, width), lambda h: (0, 0, 0)),
            pl.BlockSpec((rows, lanes), lambda h: (0, h)),
        ],
        out_specs=pl.BlockSpec((rows, lanes), lambda h: (0, h)),
        out_shape=jax.ShapeDtypeStruct((rows, width), jnp.bfloat16),
        compiler_params=params,
    )(probs_c, probs_d, recv_v, draft_value)


def feed_forward(rows_in, ln_gain, w_in, w_out):
    inner = w_out.shape[0]
    floats = rows_in.astype(jnp.float32)
    mean_value = jnp.mean(floats, axis=1, keepdims=True)
    centred = floats - mean_value
    variance = jnp.mean(centred * centred, axis=1, keepdims=True)
    normed = (centred * lax.rsqrt(variance + 1e-05) * ln_gain.astype(jnp.float32)[None, :]).astype(
        jnp.bfloat16
    )
    both = jnp.dot(normed, w_in, preferred_element_type=jnp.float32)
    middle = (jax.nn.gelu(both[:, :inner], approximate=False) * both[:, inner:]).astype(
        jnp.bfloat16
    )
    return jnp.dot(middle, w_out, preferred_element_type=jnp.float32).astype(jnp.bfloat16)


def local(
    hidden,
    draft_query,
    draft_key,
    draft_value,
    cache_keys,
    cache_values,
    page_target,
    page_slot,
    page_fill,
    tree_parent,
    tree_size,
    accepted_leaf,
    w_attn_out,
    ln_gain,
    w_in,
    w_out,
):
    devices = lax.axis_size("req")
    pages_here, page_len, width = cache_keys.shape
    per_target = max(2, -(-pages_here // devices))
    target = page_target[:, 0]
    onehot = (target[:, None] == jnp.arange(devices, dtype=jnp.int32)[None, :]).astype(jnp.int32)
    within = jnp.sum(jnp.cumsum(onehot, axis=0) * onehot, axis=1) - 1
    dest_slot = target * per_target + within
    slot_count = devices * per_target
    matches = dest_slot[None, :] == jnp.arange(slot_count, dtype=jnp.int32)[:, None]
    filled = jnp.any(matches, axis=1)
    source = jnp.sum(
        jnp.where(matches, jnp.arange(pages_here, dtype=jnp.int32)[None, :], 0), axis=1
    )
    send_fill = jnp.sum(jnp.where(matches, page_fill[None, :], 0), axis=1)
    send_owner = jnp.sum(jnp.where(matches, page_slot[None, :], 0), axis=1)
    send_meta = jnp.stack([send_fill, send_owner], axis=1).reshape(devices, per_target * 2)
    recv_k = lax.all_to_all(
        cache_keys[source].reshape(devices, per_target, page_len, width), "req", 0, 0, tiled=True
    ).reshape(slot_count, page_len, width)
    recv_v = lax.all_to_all(
        cache_values[source].reshape(devices, per_target, page_len, width), "req", 0, 0, tiled=True
    ).reshape(slot_count, page_len, width)
    recv_meta = lax.all_to_all(send_meta, "req", 0, 0, tiled=True).reshape(slot_count, 2)
    recv_fill = recv_meta[:, 0]
    recv_owner = recv_meta[:, 1]
    requests, tree_width = tree_parent.shape
    rows = requests * tree_width
    ancestors = ancestor_closure(tree_parent)
    depth = (jnp.sum(ancestors, axis=2) - 1.0).astype(jnp.int32)
    request_ids = jnp.arange(requests, dtype=jnp.int32)
    cache_len = jnp.sum(
        jnp.where(recv_owner[None, :] == request_ids[:, None], recv_fill[None, :], 0), axis=1
    )
    positions = (cache_len[:, None] + depth).reshape(rows)
    query_rot = rotate_positions(draft_query, positions, HEADS)
    key_rot = rotate_positions(draft_key, positions, HEADS)
    key_owner = jnp.where(
        jnp.arange(page_len, dtype=jnp.int32)[None, :] < recv_fill[:, None], recv_owner[:, None], -1
    ).reshape(1, -1)
    tree_mask = (
        ancestors[:, :, None, :] * jnp.eye(requests, dtype=jnp.float32)[:, None, :, None]
    ).reshape(rows, rows)
    context = attend(query_rot, recv_k, recv_v, key_rot, draft_value, key_owner, tree_mask, tree_width)
    attended = (
        hidden.astype(jnp.float32)
        + jnp.dot(context, w_attn_out, preferred_element_type=jnp.float32)
    ).astype(jnp.bfloat16)
    alive_mask = (jnp.arange(tree_width, dtype=jnp.int32)[None, :] < tree_size[:, None]).reshape(
        rows
    )
    ffn_out = feed_forward(attended, ln_gain, w_in, w_out)
    layer_out = jnp.where(
        alive_mask[:, None], attended.astype(jnp.float32) + ffn_out.astype(jnp.float32), 0.0
    ).astype(jnp.bfloat16)
    leaf_index = jnp.minimum(accepted_leaf, tree_size - 1)
    leaf_onehot = (jnp.arange(tree_width, dtype=jnp.int32)[None, :] == leaf_index[:, None]).astype(
        jnp.float32
    )
    path = jnp.einsum("ri,rij->rj", leaf_onehot, ancestors, precision=lax.Precision.HIGHEST)
    select = (
        path[:, None, :]
        * (depth[:, None, :] == jnp.arange(tree_width, dtype=jnp.int32)[None, :, None]).astype(
            jnp.float32
        )
    ).astype(jnp.bfloat16)
    kept_keys = jnp.einsum(
        "rkj,rjd->rkd",
        select,
        key_rot.reshape(requests, tree_width, width),
        preferred_element_type=jnp.float32,
    )
    kept_values = jnp.einsum(
        "rkj,rjd->rkd",
        select,
        draft_value.reshape(requests, tree_width, width),
        preferred_element_type=jnp.float32,
    )
    return (
        layer_out,
        kept_keys.reshape(rows, width).astype(jnp.bfloat16),
        kept_values.reshape(rows, width).astype(jnp.bfloat16),
    )


def solution(mesh):
    placed = (
        P("req", None),
        P("req", None),
        P("req", None),
        P("req", None),
        P("req", None, None),
        P("req", None, None),
        P("req", None),
        P("req"),
        P("req"),
        P("req", None),
        P("req"),
        P("req"),
        P(),
        P(),
        P(),
        P(),
    )
    return jax.shard_map(
        local,
        mesh=mesh,
        in_specs=placed,
        out_specs=(P("req", None), P("req", None), P("req", None)),
        check_vma=False,
    )
```

```python
import functools

import jax
import jax.numpy as jnp
from jax import lax
from jax.experimental import pallas as pl
from jax.experimental.pallas import tpu as pltpu
from jax.sharding import PartitionSpec as P

HEADS = 16


def ancestor_closure(tree_parent):
    width = tree_parent.shape[1]
    ident = jnp.eye(width, dtype=jnp.float32)
    ancestors = (
        tree_parent[:, :, None] == jnp.arange(width, dtype=jnp.int32)[None, None, :]
    ).astype(jnp.float32) + ident
    for repeat in range((width - 1).bit_length()):
        ancestors = jnp.minimum(
            jnp.einsum("rij,rjk->rik", ancestors, ancestors, precision=lax.Precision.HIGHEST), 1.0
        )
    return ancestors


def rotate_positions(values, positions, heads):
    rows, width = values.shape
    head_size = width // heads
    half = head_size // 2
    inverse = jnp.power(160000.0, -(2.0 * jnp.arange(half, dtype=jnp.float32)) / head_size)
    angle = positions.astype(jnp.float32)[:, None] * inverse[None, :]
    cosine = jnp.cos(angle)[:, None, :]
    sine = jnp.sin(angle)[:, None, :]
    shaped = values.astype(jnp.float32).reshape(rows, heads, head_size)
    first = shaped[..., :half]
    second = shaped[..., half:]
    turned = jnp.concatenate(
        [first * cosine - second * sine, second * cosine + first * sine], axis=-1
    )
    return turned.reshape(rows, width).astype(jnp.bfloat16)


def _probs_kernel(q_ref, kc_ref, kd_ref, kown_ref, tmask_ref, pc_ref, pd_ref, *,
                  tree_width, head_size, scale):
    rows, lanes = q_ref.shape
    q = q_ref[...]
    kc = kc_ref[...].reshape(-1, lanes)
    kd = kd_ref[...]
    lane = lax.broadcasted_iota(jnp.int32, (1, lanes), 1)
    qown = lax.broadcasted_iota(jnp.int32, (rows, 1), 0) // tree_width
    cmask = qown == kown_ref[...]
    tmask = tmask_ref[...] > 0.5
    dims = (((1,), (1,)), ((), ()))
    for part in range(lanes // head_size):
        sel = (lane >= part * head_size) & (lane < (part + 1) * head_size)
        qh = jnp.where(sel, q, jnp.zeros((), q.dtype))
        sc = lax.dot_general(qh, kc, dims, preferred_element_type=jnp.float32) * scale
        sd = lax.dot_general(qh, kd, dims, preferred_element_type=jnp.float32) * scale
        sc = jnp.where(cmask, sc, -1e30)
        sd = jnp.where(tmask, sd, -1e30)
        top = jnp.maximum(jnp.max(sc, axis=1, keepdims=True), jnp.max(sd, axis=1, keepdims=True))
        pc = jnp.exp(sc - top)
        pd = jnp.exp(sd - top)
        inv = 1.0 / (jnp.sum(pc, axis=1, keepdims=True) + jnp.sum(pd, axis=1, keepdims=True))
        pc_ref[part] = (pc * inv).astype(pc_ref.dtype)
        pd_ref[part] = (pd * inv).astype(pd_ref.dtype)


def _context_kernel(pc_ref, pd_ref, vc_ref, vd_ref, o_ref, *, head_size):
    rows, lanes = o_ref.shape
    vc = vc_ref[...].reshape(-1, lanes)
    vd = vd_ref[...]
    lane = lax.broadcasted_iota(jnp.int32, (1, lanes), 1)
    result = None
    for part in range(lanes // head_size):
        ctx = jnp.dot(pc_ref[part], vc, preferred_element_type=jnp.float32)
        ctx = ctx + jnp.dot(pd_ref[part], vd, preferred_element_type=jnp.float32)
        if result is None:
            result = ctx
        else:
            sel = (lane >= part * head_size) & (lane < (part + 1) * head_size)
            result = jnp.where(sel, ctx, result)
    o_ref[...] = result.astype(o_ref.dtype)


def attend(query_rot, recv_k, recv_v, key_rot, draft_value, key_owner, tree_mask, tree_width):
    rows, width = query_rot.shape
    head_size = width // HEADS
    lanes = 128
    per = lanes // head_size
    groups = width // lanes
    slots, page_len, _ = recv_k.shape
    keys = slots * page_len
    params = pltpu.CompilerParams(vmem_limit_bytes=60 * 1024 * 1024)
    probs_c, probs_d = pl.pallas_call(
        functools.partial(
            _probs_kernel, tree_width=tree_width, head_size=head_size, scale=1.0 / head_size**0.5
        ),
        grid=(groups,),
        in_specs=[
            pl.BlockSpec((rows, lanes), lambda h: (0, h)),
            pl.BlockSpec((slots, page_len, lanes), lambda h: (0, 0, h)),
            pl.BlockSpec((rows, lanes), lambda h: (0, h)),
            pl.BlockSpec((1, keys), lambda h: (0, 0)),
            pl.BlockSpec((rows, rows), lambda h: (0, 0)),
        ],
        out_specs=[
            pl.BlockSpec((None, per, rows, keys), lambda h: (h, 0, 0, 0)),
            pl.BlockSpec((None, per, rows, rows), lambda h: (h, 0, 0, 0)),
        ],
        out_shape=[
            jax.ShapeDtypeStruct((groups, per, rows, keys), jnp.bfloat16),
            jax.ShapeDtypeStruct((groups, per, rows, rows), jnp.bfloat16),
        ],
        compiler_params=params,
    )(query_rot, recv_k, key_rot, key_owner, tree_mask)
    return pl.pallas_call(
        functools.partial(_context_kernel, head_size=head_size),
        grid=(groups,),
        in_specs=[
            pl.BlockSpec((None, per, rows, keys), lambda h: (h, 0, 0, 0)),
            pl.BlockSpec((None, per, rows, rows), lambda h: (h, 0, 0, 0)),
            pl.BlockSpec((slots, page_len, lanes), lambda h: (0, 0, h)),
            pl.BlockSpec((rows, lanes), lambda h: (0, h)),
        ],
        out_specs=pl.BlockSpec((rows, lanes), lambda h: (0, h)),
        out_shape=jax.ShapeDtypeStruct((rows, width), jnp.bfloat16),
        compiler_params=params,
    )(probs_c, probs_d, recv_v, draft_value)


def feed_forward(rows_in, ln_gain, w_in, w_out):
    inner = w_out.shape[0]
    floats = rows_in.astype(jnp.float32)
    mean_value = jnp.mean(floats, axis=1, keepdims=True)
    centred = floats - mean_value
    variance = jnp.mean(centred * centred, axis=1, keepdims=True)
    normed = (centred * lax.rsqrt(variance + 1e-05) * ln_gain.astype(jnp.float32)[None, :]).astype(
        jnp.bfloat16
    )
    both = jnp.dot(normed, w_in, preferred_element_type=jnp.float32)
    middle = (jax.nn.gelu(both[:, :inner], approximate=False) * both[:, inner:]).astype(
        jnp.bfloat16
    )
    return jnp.dot(middle, w_out, preferred_element_type=jnp.float32).astype(jnp.bfloat16)


def local(
    hidden,
    draft_query,
    draft_key,
    draft_value,
    cache_keys,
    cache_values,
    page_target,
    page_slot,
    page_fill,
    tree_parent,
    tree_size,
    accepted_leaf,
    w_attn_out,
    ln_gain,
    w_in,
    w_out,
):
    devices = lax.axis_size("req")
    pages_here, page_len, width = cache_keys.shape
    per_target = max(2, -(-pages_here // devices))
    target = page_target[:, 0]
    onehot = (target[:, None] == jnp.arange(devices, dtype=jnp.int32)[None, :]).astype(jnp.int32)
    within = jnp.sum(jnp.cumsum(onehot, axis=0) * onehot, axis=1) - 1
    dest_slot = target * per_target + within
    slot_count = devices * per_target
    matches = dest_slot[None, :] == jnp.arange(slot_count, dtype=jnp.int32)[:, None]
    filled = jnp.any(matches, axis=1)
    source = jnp.sum(
        jnp.where(matches, jnp.arange(pages_here, dtype=jnp.int32)[None, :], 0), axis=1
    )
    send_fill = jnp.sum(jnp.where(matches, page_fill[None, :], 0), axis=1)
    send_owner = jnp.sum(jnp.where(matches, page_slot[None, :], 0), axis=1)
    send_meta = jnp.stack([send_fill, send_owner], axis=1).reshape(devices, per_target * 2)
    recv_k = lax.all_to_all(
        cache_keys[source].reshape(devices, per_target, page_len, width), "req", 0, 0, tiled=True
    ).reshape(slot_count, page_len, width)
    recv_v = lax.all_to_all(
        cache_values[source].reshape(devices, per_target, page_len, width), "req", 0, 0, tiled=True
    ).reshape(slot_count, page_len, width)
    recv_meta = lax.all_to_all(send_meta, "req", 0, 0, tiled=True).reshape(slot_count, 2)
    recv_fill = recv_meta[:, 0]
    recv_owner = recv_meta[:, 1]
    requests, tree_width = tree_parent.shape
    rows = requests * tree_width
    ancestors = ancestor_closure(tree_parent)
    depth = (jnp.sum(ancestors, axis=2) - 1.0).astype(jnp.int32)
    request_ids = jnp.arange(requests, dtype=jnp.int32)
    cache_len = jnp.sum(
        jnp.where(recv_owner[None, :] == request_ids[:, None], recv_fill[None, :], 0), axis=1
    )
    positions = (cache_len[:, None] + depth).reshape(rows)
    query_rot = rotate_positions(draft_query, positions, HEADS)
    key_rot = rotate_positions(draft_key, positions, HEADS)
    key_owner = jnp.where(
        jnp.arange(page_len, dtype=jnp.int32)[None, :] < recv_fill[:, None], recv_owner[:, None], -1
    ).reshape(1, -1)
    tree_mask = (
        ancestors[:, :, None, :] * jnp.eye(requests, dtype=jnp.float32)[:, None, :, None]
    ).reshape(rows, rows)
    context = attend(query_rot, recv_k, recv_v, key_rot, draft_value, key_owner, tree_mask, tree_width)
    attended = (
        hidden.astype(jnp.float32)
        + jnp.dot(context, w_attn_out, preferred_element_type=jnp.float32)
    ).astype(jnp.bfloat16)
    alive_mask = (jnp.arange(tree_width, dtype=jnp.int32)[None, :] < tree_size[:, None]).reshape(
        rows
    )
    ffn_out = feed_forward(attended, ln_gain, w_in, w_out)
    layer_out = jnp.where(
        alive_mask[:, None], attended.astype(jnp.float32) + ffn_out.astype(jnp.float32), 0.0
    ).astype(jnp.bfloat16)
    leaf_index = jnp.minimum(accepted_leaf, tree_size - 1)
    leaf_onehot = (jnp.arange(tree_width, dtype=jnp.int32)[None, :] == leaf_index[:, None]).astype(
        jnp.float32
    )
    path = jnp.einsum("ri,rij->rj", leaf_onehot, ancestors, precision=lax.Precision.HIGHEST)
    select = (
        path[:, None, :]
        * (depth[:, None, :] == jnp.arange(tree_width, dtype=jnp.int32)[None, :, None]).astype(
            jnp.float32
        )
    ).astype(jnp.bfloat16)
    kept_keys = jnp.einsum(
        "rkj,rjd->rkd",
        select,
        key_rot.reshape(requests, tree_width, width),
        preferred_element_type=jnp.float32,
    )
    kept_values = jnp.einsum(
        "rkj,rjd->rkd",
        select,
        draft_value.reshape(requests, tree_width, width),
        preferred_element_type=jnp.float32,
    )
    return (
        layer_out,
        kept_keys.reshape(rows, width).astype(jnp.bfloat16),
        kept_values.reshape(rows, width).astype(jnp.bfloat16),
    )


def solution(mesh):
    placed = (
        P("req", None),
        P("req", None),
        P("req", None),
        P("req", None),
        P("req", None, None),
        P("req", None, None),
        P("req", None),
        P("req"),
        P("req"),
        P("req", None),
        P("req"),
        P("req"),
        P(),
        P(),
        P(),
        P(),
    )
    return jax.shard_map(
        local,
        mesh=mesh,
        in_specs=placed,
        out_specs=(P("req", None), P("req", None), P("req", None)),
        check_vma=False,
    )
```

```python
import functools

import jax
import jax.numpy as jnp
from jax import lax
from jax.experimental import pallas as pl
from jax.experimental.pallas import tpu as pltpu
from jax.sharding import PartitionSpec as P

HEADS = 16


def ancestor_closure(tree_parent):
    width = tree_parent.shape[1]
    ident = jnp.eye(width, dtype=jnp.float32)
    ancestors = (
        tree_parent[:, :, None] == jnp.arange(width, dtype=jnp.int32)[None, None, :]
    ).astype(jnp.float32) + ident
    for repeat in range((width - 1).bit_length()):
        ancestors = jnp.minimum(
            jnp.einsum("rij,rjk->rik", ancestors, ancestors, precision=lax.Precision.HIGHEST), 1.0
        )
    return ancestors


def rotate_positions(values, positions, heads):
    rows, width = values.shape
    head_size = width // heads
    half = head_size // 2
    inverse = jnp.power(160000.0, -(2.0 * jnp.arange(half, dtype=jnp.float32)) / head_size)
    angle = positions.astype(jnp.float32)[:, None] * inverse[None, :]
    cosine = jnp.cos(angle)[:, None, :]
    sine = jnp.sin(angle)[:, None, :]
    shaped = values.astype(jnp.float32).reshape(rows, heads, head_size)
    first = shaped[..., :half]
    second = shaped[..., half:]
    turned = jnp.concatenate(
        [first * cosine - second * sine, second * cosine + first * sine], axis=-1
    )
    return turned.reshape(rows, width).astype(jnp.bfloat16)


def _probs_kernel(q_ref, kc_ref, kd_ref, kown_ref, tmask_ref, pc_ref, pd_ref, *,
                  tree_width, head_size, scale):
    rows, lanes = q_ref.shape
    q = q_ref[...]
    kc = kc_ref[...].reshape(-1, lanes)
    kd = kd_ref[...]
    lane = lax.broadcasted_iota(jnp.int32, (1, lanes), 1)
    qown = lax.broadcasted_iota(jnp.int32, (rows, 1), 0) // tree_width
    cmask = qown == kown_ref[...]
    tmask = tmask_ref[...] > 0.5
    dims = (((1,), (1,)), ((), ()))
    for part in range(lanes // head_size):
        sel = (lane >= part * head_size) & (lane < (part + 1) * head_size)
        qh = jnp.where(sel, q, jnp.zeros((), q.dtype))
        sc = lax.dot_general(qh, kc, dims, preferred_element_type=jnp.float32) * scale
        sd = lax.dot_general(qh, kd, dims, preferred_element_type=jnp.float32) * scale
        sc = jnp.where(cmask, sc, -1e30)
        sd = jnp.where(tmask, sd, -1e30)
        top = jnp.maximum(jnp.max(sc, axis=1, keepdims=True), jnp.max(sd, axis=1, keepdims=True))
        pc = jnp.exp(sc - top)
        pd = jnp.exp(sd - top)
        inv = 1.0 / (jnp.sum(pc, axis=1, keepdims=True) + jnp.sum(pd, axis=1, keepdims=True))
        pc_ref[part] = (pc * inv).astype(pc_ref.dtype)
        pd_ref[part] = (pd * inv).astype(pd_ref.dtype)


def _context_kernel(pc_ref, pd_ref, vc_ref, vd_ref, o_ref, *, head_size):
    rows, lanes = o_ref.shape
    vc = vc_ref[...].reshape(-1, lanes)
    vd = vd_ref[...]
    lane = lax.broadcasted_iota(jnp.int32, (1, lanes), 1)
    result = None
    for part in range(lanes // head_size):
        ctx = jnp.dot(pc_ref[part], vc, preferred_element_type=jnp.float32)
        ctx = ctx + jnp.dot(pd_ref[part], vd, preferred_element_type=jnp.float32)
        if result is None:
            result = ctx
        else:
            sel = (lane >= part * head_size) & (lane < (part + 1) * head_size)
            result = jnp.where(sel, ctx, result)
    o_ref[...] = result.astype(o_ref.dtype)


def attend(query_rot, recv_k, recv_v, key_rot, draft_value, key_owner, tree_mask, tree_width):
    rows, width = query_rot.shape
    head_size = width // HEADS
    lanes = 128
    per = lanes // head_size
    groups = width // lanes
    slots, page_len, _ = recv_k.shape
    keys = slots * page_len
    params = pltpu.CompilerParams(vmem_limit_bytes=60 * 1024 * 1024)
    probs_c, probs_d = pl.pallas_call(
        functools.partial(
            _probs_kernel, tree_width=tree_width, head_size=head_size, scale=1.0 / head_size**0.5
        ),
        grid=(groups,),
        in_specs=[
            pl.BlockSpec((rows, lanes), lambda h: (0, h)),
            pl.BlockSpec((slots, page_len, lanes), lambda h: (0, 0, h)),
            pl.BlockSpec((rows, lanes), lambda h: (0, h)),
            pl.BlockSpec((1, keys), lambda h: (0, 0)),
            pl.BlockSpec((rows, rows), lambda h: (0, 0)),
        ],
        out_specs=[
            pl.BlockSpec((None, per, rows, keys), lambda h: (h, 0, 0, 0)),
            pl.BlockSpec((None, per, rows, rows), lambda h: (h, 0, 0, 0)),
        ],
        out_shape=[
            jax.ShapeDtypeStruct((groups, per, rows, keys), jnp.bfloat16),
            jax.ShapeDtypeStruct((groups, per, rows, rows), jnp.bfloat16),
        ],
        compiler_params=params,
    )(query_rot, recv_k, key_rot, key_owner, tree_mask)
    return pl.pallas_call(
        functools.partial(_context_kernel, head_size=head_size),
        grid=(groups,),
        in_specs=[
            pl.BlockSpec((None, per, rows, keys), lambda h: (h, 0, 0, 0)),
            pl.BlockSpec((None, per, rows, rows), lambda h: (h, 0, 0, 0)),
            pl.BlockSpec((slots, page_len, lanes), lambda h: (0, 0, h)),
            pl.BlockSpec((rows, lanes), lambda h: (0, h)),
        ],
        out_specs=pl.BlockSpec((rows, lanes), lambda h: (0, h)),
        out_shape=jax.ShapeDtypeStruct((rows, width), jnp.bfloat16),
        compiler_params=params,
    )(probs_c, probs_d, recv_v, draft_value)


def feed_forward(rows_in, ln_gain, w_in, w_out):
    inner = w_out.shape[0]
    floats = rows_in.astype(jnp.float32)
    mean_value = jnp.mean(floats, axis=1, keepdims=True)
    centred = floats - mean_value
    variance = jnp.mean(centred * centred, axis=1, keepdims=True)
    normed = (centred * lax.rsqrt(variance + 1e-05) * ln_gain.astype(jnp.float32)[None, :]).astype(
        jnp.bfloat16
    )
    normed = lax.optimization_barrier(normed)
    both = jnp.dot(normed, w_in, preferred_element_type=jnp.float32)
    middle = (jax.nn.gelu(both[:, :inner], approximate=False) * both[:, inner:]).astype(
        jnp.bfloat16
    )
    middle = lax.optimization_barrier(middle)
    return jnp.dot(middle, w_out, preferred_element_type=jnp.float32).astype(jnp.bfloat16)


def local(
    hidden,
    draft_query,
    draft_key,
    draft_value,
    cache_keys,
    cache_values,
    page_target,
    page_slot,
    page_fill,
    tree_parent,
    tree_size,
    accepted_leaf,
    w_attn_out,
    ln_gain,
    w_in,
    w_out,
):
    devices = lax.axis_size("req")
    pages_here, page_len, width = cache_keys.shape
    per_target = max(2, -(-pages_here // devices))
    target = page_target[:, 0]
    onehot = (target[:, None] == jnp.arange(devices, dtype=jnp.int32)[None, :]).astype(jnp.int32)
    within = jnp.sum(jnp.cumsum(onehot, axis=0) * onehot, axis=1) - 1
    dest_slot = target * per_target + within
    slot_count = devices * per_target
    matches = dest_slot[None, :] == jnp.arange(slot_count, dtype=jnp.int32)[:, None]
    filled = jnp.any(matches, axis=1)
    source = jnp.sum(
        jnp.where(matches, jnp.arange(pages_here, dtype=jnp.int32)[None, :], 0), axis=1
    )
    send_fill = jnp.sum(jnp.where(matches, page_fill[None, :], 0), axis=1)
    send_owner = jnp.sum(jnp.where(matches, page_slot[None, :], 0), axis=1)
    send_meta = jnp.stack([send_fill, send_owner], axis=1).reshape(devices, per_target * 2)
    recv_k = lax.all_to_all(
        cache_keys[source].reshape(devices, per_target, page_len, width), "req", 0, 0, tiled=True
    ).reshape(slot_count, page_len, width)
    recv_v = lax.all_to_all(
        cache_values[source].reshape(devices, per_target, page_len, width), "req", 0, 0, tiled=True
    ).reshape(slot_count, page_len, width)
    recv_meta = lax.all_to_all(send_meta, "req", 0, 0, tiled=True).reshape(slot_count, 2)
    recv_fill = recv_meta[:, 0]
    recv_owner = recv_meta[:, 1]
    requests, tree_width = tree_parent.shape
    rows = requests * tree_width
    ancestors = ancestor_closure(tree_parent)
    depth = (jnp.sum(ancestors, axis=2) - 1.0).astype(jnp.int32)
    request_ids = jnp.arange(requests, dtype=jnp.int32)
    cache_len = jnp.sum(
        jnp.where(recv_owner[None, :] == request_ids[:, None], recv_fill[None, :], 0), axis=1
    )
    positions = (cache_len[:, None] + depth).reshape(rows)
    query_rot = rotate_positions(draft_query, positions, HEADS)
    key_rot = rotate_positions(draft_key, positions, HEADS)
    key_owner = jnp.where(
        jnp.arange(page_len, dtype=jnp.int32)[None, :] < recv_fill[:, None], recv_owner[:, None], -1
    ).reshape(1, -1)
    tree_mask = (
        ancestors[:, :, None, :] * jnp.eye(requests, dtype=jnp.float32)[:, None, :, None]
    ).reshape(rows, rows)
    context = attend(query_rot, recv_k, recv_v, key_rot, draft_value, key_owner, tree_mask, tree_width)
    attended = (
        hidden.astype(jnp.float32)
        + jnp.dot(context, w_attn_out, preferred_element_type=jnp.float32)
    ).astype(jnp.bfloat16)
    alive_mask = (jnp.arange(tree_width, dtype=jnp.int32)[None, :] < tree_size[:, None]).reshape(
        rows
    )
    ffn_out = feed_forward(attended, ln_gain, w_in, w_out)
    layer_out = jnp.where(
        alive_mask[:, None], attended.astype(jnp.float32) + ffn_out.astype(jnp.float32), 0.0
    ).astype(jnp.bfloat16)
    leaf_index = jnp.minimum(accepted_leaf, tree_size - 1)
    leaf_onehot = (jnp.arange(tree_width, dtype=jnp.int32)[None, :] == leaf_index[:, None]).astype(
        jnp.float32
    )
    path = jnp.einsum("ri,rij->rj", leaf_onehot, ancestors, precision=lax.Precision.HIGHEST)
    select = (
        path[:, None, :]
        * (depth[:, None, :] == jnp.arange(tree_width, dtype=jnp.int32)[None, :, None]).astype(
            jnp.float32
        )
    ).astype(jnp.bfloat16)
    kept_keys = jnp.einsum(
        "rkj,rjd->rkd",
        select,
        key_rot.reshape(requests, tree_width, width),
        preferred_element_type=jnp.float32,
    )
    kept_values = jnp.einsum(
        "rkj,rjd->rkd",
        select,
        draft_value.reshape(requests, tree_width, width),
        preferred_element_type=jnp.float32,
    )
    return (
        layer_out,
        kept_keys.reshape(rows, width).astype(jnp.bfloat16),
        kept_values.reshape(rows, width).astype(jnp.bfloat16),
    )


def solution(mesh):
    placed = (
        P("req", None),
        P("req", None),
        P("req", None),
        P("req", None),
        P("req", None, None),
        P("req", None, None),
        P("req", None),
        P("req"),
        P("req"),
        P("req", None),
        P("req"),
        P("req"),
        P(),
        P(),
        P(),
        P(),
    )
    return jax.shard_map(
        local,
        mesh=mesh,
        in_specs=placed,
        out_specs=(P("req", None), P("req", None), P("req", None)),
        check_vma=False,
    )
```

```python
import functools

import jax
import jax.numpy as jnp
from jax import lax
from jax.experimental import pallas as pl
from jax.experimental.pallas import tpu as pltpu
from jax.sharding import PartitionSpec as P

HEADS = 16


def ancestor_closure(tree_parent):
    width = tree_parent.shape[1]
    ident = jnp.eye(width, dtype=jnp.float32)
    ancestors = (
        tree_parent[:, :, None] == jnp.arange(width, dtype=jnp.int32)[None, None, :]
    ).astype(jnp.float32) + ident
    for repeat in range((width - 1).bit_length()):
        ancestors = jnp.minimum(
            jnp.einsum("rij,rjk->rik", ancestors, ancestors, precision=lax.Precision.HIGHEST), 1.0
        )
    return ancestors


def rotate_positions(values, positions, heads):
    rows, width = values.shape
    head_size = width // heads
    half = head_size // 2
    inverse = jnp.power(160000.0, -(2.0 * jnp.arange(half, dtype=jnp.float32)) / head_size)
    angle = positions.astype(jnp.float32)[:, None] * inverse[None, :]
    cosine = jnp.cos(angle)[:, None, :]
    sine = jnp.sin(angle)[:, None, :]
    shaped = values.astype(jnp.float32).reshape(rows, heads, head_size)
    first = shaped[..., :half]
    second = shaped[..., half:]
    turned = jnp.concatenate(
        [first * cosine - second * sine, second * cosine + first * sine], axis=-1
    )
    return turned.reshape(rows, width).astype(jnp.bfloat16)


def _probs_kernel(q_ref, kc_ref, kd_ref, kown_ref, tmask_ref, pc_ref, pd_ref, *,
                  tree_width, head_size, scale):
    rows, lanes = q_ref.shape
    q = q_ref[...]
    kc = kc_ref[...].reshape(-1, lanes)
    kd = kd_ref[...]
    lane = lax.broadcasted_iota(jnp.int32, (1, lanes), 1)
    qown = lax.broadcasted_iota(jnp.int32, (rows, 1), 0) // tree_width
    cmask = qown == kown_ref[...]
    tmask = tmask_ref[...] > 0.5
    dims = (((1,), (1,)), ((), ()))
    for part in range(lanes // head_size):
        sel = (lane >= part * head_size) & (lane < (part + 1) * head_size)
        qh = jnp.where(sel, q, jnp.zeros((), q.dtype))
        sc = lax.dot_general(qh, kc, dims, preferred_element_type=jnp.float32) * scale
        sd = lax.dot_general(qh, kd, dims, preferred_element_type=jnp.float32) * scale
        sc = jnp.where(cmask, sc, -1e30)
        sd = jnp.where(tmask, sd, -1e30)
        top = jnp.maximum(jnp.max(sc, axis=1, keepdims=True), jnp.max(sd, axis=1, keepdims=True))
        pc = jnp.exp(sc - top)
        pd = jnp.exp(sd - top)
        inv = 1.0 / (jnp.sum(pc, axis=1, keepdims=True) + jnp.sum(pd, axis=1, keepdims=True))
        pc_ref[part] = (pc * inv).astype(pc_ref.dtype)
        pd_ref[part] = (pd * inv).astype(pd_ref.dtype)


def _context_kernel(pc_ref, pd_ref, vc_ref, vd_ref, o_ref, *, head_size):
    rows, lanes = o_ref.shape
    vc = vc_ref[...].reshape(-1, lanes)
    vd = vd_ref[...]
    lane = lax.broadcasted_iota(jnp.int32, (1, lanes), 1)
    result = None
    for part in range(lanes // head_size):
        ctx = jnp.dot(pc_ref[part], vc, preferred_element_type=jnp.float32)
        ctx = ctx + jnp.dot(pd_ref[part], vd, preferred_element_type=jnp.float32)
        if result is None:
            result = ctx
        else:
            sel = (lane >= part * head_size) & (lane < (part + 1) * head_size)
            result = jnp.where(sel, ctx, result)
    o_ref[...] = result.astype(o_ref.dtype)


def attend(query_rot, recv_k, recv_v, key_rot, draft_value, key_owner, tree_mask, tree_width):
    rows, width = query_rot.shape
    head_size = width // HEADS
    lanes = 128
    per = lanes // head_size
    groups = width // lanes
    slots, page_len, _ = recv_k.shape
    keys = slots * page_len
    params = pltpu.CompilerParams(vmem_limit_bytes=60 * 1024 * 1024)
    probs_c, probs_d = pl.pallas_call(
        functools.partial(
            _probs_kernel, tree_width=tree_width, head_size=head_size, scale=1.0 / head_size**0.5
        ),
        grid=(groups,),
        in_specs=[
            pl.BlockSpec((rows, lanes), lambda h: (0, h)),
            pl.BlockSpec((slots, page_len, lanes), lambda h: (0, 0, h)),
            pl.BlockSpec((rows, lanes), lambda h: (0, h)),
            pl.BlockSpec((1, keys), lambda h: (0, 0)),
            pl.BlockSpec((rows, rows), lambda h: (0, 0)),
        ],
        out_specs=[
            pl.BlockSpec((None, per, rows, keys), lambda h: (h, 0, 0, 0)),
            pl.BlockSpec((None, per, rows, rows), lambda h: (h, 0, 0, 0)),
        ],
        out_shape=[
            jax.ShapeDtypeStruct((groups, per, rows, keys), jnp.bfloat16),
            jax.ShapeDtypeStruct((groups, per, rows, rows), jnp.bfloat16),
        ],
        compiler_params=params,
    )(query_rot, recv_k, key_rot, key_owner, tree_mask)
    return pl.pallas_call(
        functools.partial(_context_kernel, head_size=head_size),
        grid=(groups,),
        in_specs=[
            pl.BlockSpec((None, per, rows, keys), lambda h: (h, 0, 0, 0)),
            pl.BlockSpec((None, per, rows, rows), lambda h: (h, 0, 0, 0)),
            pl.BlockSpec((slots, page_len, lanes), lambda h: (0, 0, h)),
            pl.BlockSpec((rows, lanes), lambda h: (0, h)),
        ],
        out_specs=pl.BlockSpec((rows, lanes), lambda h: (0, h)),
        out_shape=jax.ShapeDtypeStruct((rows, width), jnp.bfloat16),
        compiler_params=params,
    )(probs_c, probs_d, recv_v, draft_value)


def feed_forward(rows_in, ln_gain, w_in, w_out):
    inner = w_out.shape[0]
    floats = rows_in.astype(jnp.float32)
    mean_value = jnp.mean(floats, axis=1, keepdims=True)
    centred = floats - mean_value
    variance = jnp.mean(centred * centred, axis=1, keepdims=True)
    normed = (centred * lax.rsqrt(variance + 1e-05) * ln_gain.astype(jnp.float32)[None, :]).astype(
        jnp.bfloat16
    )
    both = jnp.dot(normed, w_in, preferred_element_type=jnp.float32)
    middle = (jax.nn.gelu(both[:, :inner], approximate=False) * both[:, inner:]).astype(
        jnp.bfloat16
    )
    return jnp.dot(middle, w_out, preferred_element_type=jnp.float32).astype(jnp.bfloat16)


def local(
    hidden,
    draft_query,
    draft_key,
    draft_value,
    cache_keys,
    cache_values,
    page_target,
    page_slot,
    page_fill,
    tree_parent,
    tree_size,
    accepted_leaf,
    w_attn_out,
    ln_gain,
    w_in,
    w_out,
):
    devices = lax.axis_size("req")
    pages_here, page_len, width = cache_keys.shape
    per_target = max(2, -(-pages_here // devices))
    target = page_target[:, 0]
    onehot = (target[:, None] == jnp.arange(devices, dtype=jnp.int32)[None, :]).astype(jnp.int32)
    within = jnp.sum(jnp.cumsum(onehot, axis=0) * onehot, axis=1) - 1
    dest_slot = target * per_target + within
    slot_count = devices * per_target
    matches = dest_slot[None, :] == jnp.arange(slot_count, dtype=jnp.int32)[:, None]
    filled = jnp.any(matches, axis=1)
    source = jnp.sum(
        jnp.where(matches, jnp.arange(pages_here, dtype=jnp.int32)[None, :], 0), axis=1
    )
    send_fill = jnp.sum(jnp.where(matches, page_fill[None, :], 0), axis=1)
    send_owner = jnp.sum(jnp.where(matches, page_slot[None, :], 0), axis=1)
    send_meta = jnp.stack([send_fill, send_owner], axis=1).reshape(devices, per_target * 2)
    send_k = cache_keys[source].reshape(devices, per_target, page_len, width)
    send_meta, send_k = lax.optimization_barrier((send_meta, send_k))
    recv_k = lax.all_to_all(send_k, "req", 0, 0, tiled=True).reshape(slot_count, page_len, width)
    recv_v = lax.all_to_all(
        cache_values[source].reshape(devices, per_target, page_len, width), "req", 0, 0, tiled=True
    ).reshape(slot_count, page_len, width)
    recv_meta = lax.all_to_all(send_meta, "req", 0, 0, tiled=True).reshape(slot_count, 2)
    recv_fill = recv_meta[:, 0]
    recv_owner = recv_meta[:, 1]
    requests, tree_width = tree_parent.shape
    rows = requests * tree_width
    ancestors = ancestor_closure(tree_parent)
    depth = (jnp.sum(ancestors, axis=2) - 1.0).astype(jnp.int32)
    request_ids = jnp.arange(requests, dtype=jnp.int32)
    cache_len = jnp.sum(
        jnp.where(recv_owner[None, :] == request_ids[:, None], recv_fill[None, :], 0), axis=1
    )
    positions = (cache_len[:, None] + depth).reshape(rows)
    query_rot = rotate_positions(draft_query, positions, HEADS)
    key_rot = rotate_positions(draft_key, positions, HEADS)
    key_owner = jnp.where(
        jnp.arange(page_len, dtype=jnp.int32)[None, :] < recv_fill[:, None], recv_owner[:, None], -1
    ).reshape(1, -1)
    tree_mask = (
        ancestors[:, :, None, :] * jnp.eye(requests, dtype=jnp.float32)[:, None, :, None]
    ).reshape(rows, rows)
    context = attend(query_rot, recv_k, recv_v, key_rot, draft_value, key_owner, tree_mask, tree_width)
    attended = (
        hidden.astype(jnp.float32)
        + jnp.dot(context, w_attn_out, preferred_element_type=jnp.float32)
    ).astype(jnp.bfloat16)
    alive_mask = (jnp.arange(tree_width, dtype=jnp.int32)[None, :] < tree_size[:, None]).reshape(
        rows
    )
    ffn_out = feed_forward(attended, ln_gain, w_in, w_out)
    layer_out = jnp.where(
        alive_mask[:, None], attended.astype(jnp.float32) + ffn_out.astype(jnp.float32), 0.0
    ).astype(jnp.bfloat16)
    leaf_index = jnp.minimum(accepted_leaf, tree_size - 1)
    leaf_onehot = (jnp.arange(tree_width, dtype=jnp.int32)[None, :] == leaf_index[:, None]).astype(
        jnp.float32
    )
    path = jnp.einsum("ri,rij->rj", leaf_onehot, ancestors, precision=lax.Precision.HIGHEST)
    select = (
        path[:, None, :]
        * (depth[:, None, :] == jnp.arange(tree_width, dtype=jnp.int32)[None, :, None]).astype(
            jnp.float32
        )
    ).astype(jnp.bfloat16)
    kept_keys = jnp.einsum(
        "rkj,rjd->rkd",
        select,
        key_rot.reshape(requests, tree_width, width),
        preferred_element_type=jnp.float32,
    )
    kept_values = jnp.einsum(
        "rkj,rjd->rkd",
        select,
        draft_value.reshape(requests, tree_width, width),
        preferred_element_type=jnp.float32,
    )
    return (
        layer_out,
        kept_keys.reshape(rows, width).astype(jnp.bfloat16),
        kept_values.reshape(rows, width).astype(jnp.bfloat16),
    )


def solution(mesh):
    placed = (
        P("req", None),
        P("req", None),
        P("req", None),
        P("req", None),
        P("req", None, None),
        P("req", None, None),
        P("req", None),
        P("req"),
        P("req"),
        P("req", None),
        P("req"),
        P("req"),
        P(),
        P(),
        P(),
        P(),
    )
    return jax.shard_map(
        local,
        mesh=mesh,
        in_specs=placed,
        out_specs=(P("req", None), P("req", None), P("req", None)),
        check_vma=False,
    )
```

```python
import functools

import jax
import jax.numpy as jnp
from jax import lax
from jax.experimental import pallas as pl
from jax.experimental.pallas import tpu as pltpu
from jax.sharding import PartitionSpec as P

HEADS = 16


def ancestor_closure(tree_parent):
    width = tree_parent.shape[1]
    ident = jnp.eye(width, dtype=jnp.float32)
    ancestors = (
        tree_parent[:, :, None] == jnp.arange(width, dtype=jnp.int32)[None, None, :]
    ).astype(jnp.float32) + ident
    for repeat in range((width - 1).bit_length()):
        ancestors = jnp.minimum(
            jnp.einsum("rij,rjk->rik", ancestors, ancestors, precision=lax.Precision.HIGHEST), 1.0
        )
    return ancestors


def rotate_positions(values, positions, heads):
    rows, width = values.shape
    head_size = width // heads
    half = head_size // 2
    inverse = jnp.power(160000.0, -(2.0 * jnp.arange(half, dtype=jnp.float32)) / head_size)
    angle = positions.astype(jnp.float32)[:, None] * inverse[None, :]
    cosine = jnp.cos(angle)[:, None, :]
    sine = jnp.sin(angle)[:, None, :]
    shaped = values.astype(jnp.float32).reshape(rows, heads, head_size)
    first = shaped[..., :half]
    second = shaped[..., half:]
    turned = jnp.concatenate(
        [first * cosine - second * sine, second * cosine + first * sine], axis=-1
    )
    return turned.reshape(rows, width).astype(jnp.bfloat16)


def _probs_kernel(q_ref, kc_ref, kd_ref, kown_ref, tmask_ref, pc_ref, pd_ref, *,
                  tree_width, head_size, scale):
    rows, lanes = q_ref.shape
    q = q_ref[...]
    kc = kc_ref[...].reshape(-1, lanes)
    kd = kd_ref[...]
    lane = lax.broadcasted_iota(jnp.int32, (1, lanes), 1)
    qown = lax.broadcasted_iota(jnp.int32, (rows, 1), 0) // tree_width
    cmask = qown == kown_ref[...]
    tmask = tmask_ref[...] > 0.5
    dims = (((1,), (1,)), ((), ()))
    for part in range(lanes // head_size):
        sel = (lane >= part * head_size) & (lane < (part + 1) * head_size)
        qh = jnp.where(sel, q, jnp.zeros((), q.dtype))
        sc = lax.dot_general(qh, kc, dims, preferred_element_type=jnp.float32) * scale
        sd = lax.dot_general(qh, kd, dims, preferred_element_type=jnp.float32) * scale
        sc = jnp.where(cmask, sc, -1e30)
        sd = jnp.where(tmask, sd, -1e30)
        top = jnp.maximum(jnp.max(sc, axis=1, keepdims=True), jnp.max(sd, axis=1, keepdims=True))
        pc = jnp.exp(sc - top)
        pd = jnp.exp(sd - top)
        inv = 1.0 / (jnp.sum(pc, axis=1, keepdims=True) + jnp.sum(pd, axis=1, keepdims=True))
        pc_ref[part] = (pc * inv).astype(pc_ref.dtype)
        pd_ref[part] = (pd * inv).astype(pd_ref.dtype)


def _context_kernel(pc_ref, pd_ref, vc_ref, vd_ref, o_ref, *, head_size):
    rows, lanes = o_ref.shape
    vc = vc_ref[...].reshape(-1, lanes)
    vd = vd_ref[...]
    lane = lax.broadcasted_iota(jnp.int32, (1, lanes), 1)
    result = None
    for part in range(lanes // head_size):
        ctx = jnp.dot(pc_ref[part], vc, preferred_element_type=jnp.float32)
        ctx = ctx + jnp.dot(pd_ref[part], vd, preferred_element_type=jnp.float32)
        if result is None:
            result = ctx
        else:
            sel = (lane >= part * head_size) & (lane < (part + 1) * head_size)
            result = jnp.where(sel, ctx, result)
    o_ref[...] = result.astype(o_ref.dtype)


def attend(query_rot, recv_k, recv_v, key_rot, draft_value, key_owner, tree_mask, tree_width):
    rows, width = query_rot.shape
    head_size = width // HEADS
    lanes = 128
    per = lanes // head_size
    groups = width // lanes
    slots, page_len, _ = recv_k.shape
    keys = slots * page_len
    params = pltpu.CompilerParams(vmem_limit_bytes=60 * 1024 * 1024)
    probs_c, probs_d = pl.pallas_call(
        functools.partial(
            _probs_kernel, tree_width=tree_width, head_size=head_size, scale=1.0 / head_size**0.5
        ),
        grid=(groups,),
        in_specs=[
            pl.BlockSpec((rows, lanes), lambda h: (0, h)),
            pl.BlockSpec((slots, page_len, lanes), lambda h: (0, 0, h)),
            pl.BlockSpec((rows, lanes), lambda h: (0, h)),
            pl.BlockSpec((1, keys), lambda h: (0, 0)),
            pl.BlockSpec((rows, rows), lambda h: (0, 0)),
        ],
        out_specs=[
            pl.BlockSpec((None, per, rows, keys), lambda h: (h, 0, 0, 0)),
            pl.BlockSpec((None, per, rows, rows), lambda h: (h, 0, 0, 0)),
        ],
        out_shape=[
            jax.ShapeDtypeStruct((groups, per, rows, keys), jnp.bfloat16),
            jax.ShapeDtypeStruct((groups, per, rows, rows), jnp.bfloat16),
        ],
        compiler_params=params,
    )(query_rot, recv_k, key_rot, key_owner, tree_mask)
    return pl.pallas_call(
        functools.partial(_context_kernel, head_size=head_size),
        grid=(groups,),
        in_specs=[
            pl.BlockSpec((None, per, rows, keys), lambda h: (h, 0, 0, 0)),
            pl.BlockSpec((None, per, rows, rows), lambda h: (h, 0, 0, 0)),
            pl.BlockSpec((slots, page_len, lanes), lambda h: (0, 0, h)),
            pl.BlockSpec((rows, lanes), lambda h: (0, h)),
        ],
        out_specs=pl.BlockSpec((rows, lanes), lambda h: (0, h)),
        out_shape=jax.ShapeDtypeStruct((rows, width), jnp.bfloat16),
        compiler_params=params,
    )(probs_c, probs_d, recv_v, draft_value)


def _ffn_kernel(x_ref, g_ref, win_ref, wout_ref, alive_ref, o_ref, *, inner):
    x = x_ref[...].astype(jnp.float32)
    mean_value = jnp.mean(x, axis=1, keepdims=True)
    centred = x - mean_value
    variance = jnp.mean(centred * centred, axis=1, keepdims=True)
    normed = (centred * lax.rsqrt(variance + 1e-05) * g_ref[...].astype(jnp.float32)).astype(
        jnp.bfloat16
    )
    both = jnp.dot(normed, win_ref[...], preferred_element_type=jnp.float32)
    gate = both[:, :inner]
    gelu = 0.5 * gate * (1.0 + lax.erf(gate * (0.5**0.5)))
    middle = (gelu * both[:, inner:]).astype(jnp.bfloat16)
    ffn = jnp.dot(middle, wout_ref[...], preferred_element_type=jnp.float32).astype(jnp.bfloat16)
    out = jnp.where(alive_ref[...] > 0, x + ffn.astype(jnp.float32), 0.0)
    o_ref[...] = out.astype(o_ref.dtype)


def feed_forward_out(attended, ln_gain, w_in, w_out, alive):
    rows, width = attended.shape
    inner = w_out.shape[0]
    whole = lambda shape: pl.BlockSpec(shape, lambda i: (0,) * len(shape))
    return pl.pallas_call(
        functools.partial(_ffn_kernel, inner=inner),
        grid=(1,),
        in_specs=[
            whole((rows, width)),
            whole((1, width)),
            whole(w_in.shape),
            whole(w_out.shape),
            whole((rows, 1)),
        ],
        out_specs=whole((rows, width)),
        out_shape=jax.ShapeDtypeStruct((rows, width), jnp.bfloat16),
        compiler_params=pltpu.CompilerParams(vmem_limit_bytes=62 * 1024 * 1024),
    )(attended, ln_gain.reshape(1, width), w_in, w_out, alive.astype(jnp.int32).reshape(rows, 1))


def local(
    hidden,
    draft_query,
    draft_key,
    draft_value,
    cache_keys,
    cache_values,
    page_target,
    page_slot,
    page_fill,
    tree_parent,
    tree_size,
    accepted_leaf,
    w_attn_out,
    ln_gain,
    w_in,
    w_out,
):
    devices = lax.axis_size("req")
    pages_here, page_len, width = cache_keys.shape
    per_target = max(2, -(-pages_here // devices))
    target = page_target[:, 0]
    onehot = (target[:, None] == jnp.arange(devices, dtype=jnp.int32)[None, :]).astype(jnp.int32)
    within = jnp.sum(jnp.cumsum(onehot, axis=0) * onehot, axis=1) - 1
    dest_slot = target * per_target + within
    slot_count = devices * per_target
    matches = dest_slot[None, :] == jnp.arange(slot_count, dtype=jnp.int32)[:, None]
    filled = jnp.any(matches, axis=1)
    source = jnp.sum(
        jnp.where(matches, jnp.arange(pages_here, dtype=jnp.int32)[None, :], 0), axis=1
    )
    send_fill = jnp.sum(jnp.where(matches, page_fill[None, :], 0), axis=1)
    send_owner = jnp.sum(jnp.where(matches, page_slot[None, :], 0), axis=1)
    send_meta = jnp.stack([send_fill, send_owner], axis=1).reshape(devices, per_target * 2)
    recv_k = lax.all_to_all(
        cache_keys[source].reshape(devices, per_target, page_len, width), "req", 0, 0, tiled=True
    ).reshape(slot_count, page_len, width)
    recv_v = lax.all_to_all(
        cache_values[source].reshape(devices, per_target, page_len, width), "req", 0, 0, tiled=True
    ).reshape(slot_count, page_len, width)
    recv_meta = lax.all_to_all(send_meta, "req", 0, 0, tiled=True).reshape(slot_count, 2)
    recv_fill = recv_meta[:, 0]
    recv_owner = recv_meta[:, 1]
    requests, tree_width = tree_parent.shape
    rows = requests * tree_width
    ancestors = ancestor_closure(tree_parent)
    depth = (jnp.sum(ancestors, axis=2) - 1.0).astype(jnp.int32)
    request_ids = jnp.arange(requests, dtype=jnp.int32)
    cache_len = jnp.sum(
        jnp.where(recv_owner[None, :] == request_ids[:, None], recv_fill[None, :], 0), axis=1
    )
    positions = (cache_len[:, None] + depth).reshape(rows)
    query_rot = rotate_positions(draft_query, positions, HEADS)
    key_rot = rotate_positions(draft_key, positions, HEADS)
    key_owner = jnp.where(
        jnp.arange(page_len, dtype=jnp.int32)[None, :] < recv_fill[:, None], recv_owner[:, None], -1
    ).reshape(1, -1)
    tree_mask = (
        ancestors[:, :, None, :] * jnp.eye(requests, dtype=jnp.float32)[:, None, :, None]
    ).reshape(rows, rows)
    context = attend(query_rot, recv_k, recv_v, key_rot, draft_value, key_owner, tree_mask, tree_width)
    attended = (
        hidden.astype(jnp.float32)
        + jnp.dot(context, w_attn_out, preferred_element_type=jnp.float32)
    ).astype(jnp.bfloat16)
    alive_mask = (jnp.arange(tree_width, dtype=jnp.int32)[None, :] < tree_size[:, None]).reshape(
        rows
    )
    layer_out = feed_forward_out(attended, ln_gain, w_in, w_out, alive_mask)
    leaf_index = jnp.minimum(accepted_leaf, tree_size - 1)
    leaf_onehot = (jnp.arange(tree_width, dtype=jnp.int32)[None, :] == leaf_index[:, None]).astype(
        jnp.float32
    )
    path = jnp.einsum("ri,rij->rj", leaf_onehot, ancestors, precision=lax.Precision.HIGHEST)
    select = (
        path[:, None, :]
        * (depth[:, None, :] == jnp.arange(tree_width, dtype=jnp.int32)[None, :, None]).astype(
            jnp.float32
        )
    ).astype(jnp.bfloat16)
    kept_keys = jnp.einsum(
        "rkj,rjd->rkd",
        select,
        key_rot.reshape(requests, tree_width, width),
        preferred_element_type=jnp.float32,
    )
    kept_values = jnp.einsum(
        "rkj,rjd->rkd",
        select,
        draft_value.reshape(requests, tree_width, width),
        preferred_element_type=jnp.float32,
    )
    return (
        layer_out,
        kept_keys.reshape(rows, width).astype(jnp.bfloat16),
        kept_values.reshape(rows, width).astype(jnp.bfloat16),
    )


def solution(mesh):
    placed = (
        P("req", None),
        P("req", None),
        P("req", None),
        P("req", None),
        P("req", None, None),
        P("req", None, None),
        P("req", None),
        P("req"),
        P("req"),
        P("req", None),
        P("req"),
        P("req"),
        P(),
        P(),
        P(),
        P(),
    )
    return jax.shard_map(
        local,
        mesh=mesh,
        in_specs=placed,
        out_specs=(P("req", None), P("req", None), P("req", None)),
        check_vma=False,
    )
```

```python
import functools

import jax
import jax.numpy as jnp
from jax import lax
from jax.experimental import pallas as pl
from jax.experimental.pallas import tpu as pltpu
from jax.sharding import PartitionSpec as P

HEADS = 16


def ancestor_closure(tree_parent):
    width = tree_parent.shape[1]
    ident = jnp.eye(width, dtype=jnp.float32)
    ancestors = (
        tree_parent[:, :, None] == jnp.arange(width, dtype=jnp.int32)[None, None, :]
    ).astype(jnp.float32) + ident
    for repeat in range((width - 1).bit_length()):
        ancestors = jnp.minimum(
            jnp.einsum("rij,rjk->rik", ancestors, ancestors, precision=lax.Precision.HIGHEST), 1.0
        )
    return ancestors


def rotate_positions(values, positions, heads):
    rows, width = values.shape
    head_size = width // heads
    half = head_size // 2
    inverse = jnp.power(160000.0, -(2.0 * jnp.arange(half, dtype=jnp.float32)) / head_size)
    angle = positions.astype(jnp.float32)[:, None] * inverse[None, :]
    cosine = jnp.cos(angle)[:, None, :]
    sine = jnp.sin(angle)[:, None, :]
    shaped = values.astype(jnp.float32).reshape(rows, heads, head_size)
    first = shaped[..., :half]
    second = shaped[..., half:]
    turned = jnp.concatenate(
        [first * cosine - second * sine, second * cosine + first * sine], axis=-1
    )
    return turned.reshape(rows, width).astype(jnp.bfloat16)


def _probs_kernel(q_ref, kc_ref, kd_ref, kown_ref, tmask_ref, pc_ref, pd_ref, *,
                  tree_width, head_size, scale):
    rows, lanes = q_ref.shape
    q = q_ref[...]
    kc = kc_ref[...].reshape(-1, lanes)
    kd = kd_ref[...]
    lane = lax.broadcasted_iota(jnp.int32, (1, lanes), 1)
    qown = lax.broadcasted_iota(jnp.int32, (rows, 1), 0) // tree_width
    cmask = qown == kown_ref[...]
    tmask = tmask_ref[...] > 0.5
    dims = (((1,), (1,)), ((), ()))
    for part in range(lanes // head_size):
        sel = (lane >= part * head_size) & (lane < (part + 1) * head_size)
        qh = jnp.where(sel, q, jnp.zeros((), q.dtype))
        sc = lax.dot_general(qh, kc, dims, preferred_element_type=jnp.float32) * scale
        sd = lax.dot_general(qh, kd, dims, preferred_element_type=jnp.float32) * scale
        sc = jnp.where(cmask, sc, -1e30)
        sd = jnp.where(tmask, sd, -1e30)
        top = jnp.maximum(jnp.max(sc, axis=1, keepdims=True), jnp.max(sd, axis=1, keepdims=True))
        pc = jnp.exp(sc - top)
        pd = jnp.exp(sd - top)
        inv = 1.0 / (jnp.sum(pc, axis=1, keepdims=True) + jnp.sum(pd, axis=1, keepdims=True))
        pc_ref[part] = (pc * inv).astype(pc_ref.dtype)
        pd_ref[part] = (pd * inv).astype(pd_ref.dtype)


def _context_kernel(pc_ref, pd_ref, vc_ref, vd_ref, o_ref, *, head_size):
    rows, lanes = o_ref.shape
    vc = vc_ref[...].reshape(-1, lanes)
    vd = vd_ref[...]
    lane = lax.broadcasted_iota(jnp.int32, (1, lanes), 1)
    result = None
    for part in range(lanes // head_size):
        ctx = jnp.dot(pc_ref[part], vc, preferred_element_type=jnp.float32)
        ctx = ctx + jnp.dot(pd_ref[part], vd, preferred_element_type=jnp.float32)
        if result is None:
            result = ctx
        else:
            sel = (lane >= part * head_size) & (lane < (part + 1) * head_size)
            result = jnp.where(sel, ctx, result)
    o_ref[...] = result.astype(o_ref.dtype)


def attend(query_rot, recv_k, recv_v, key_rot, draft_value, key_owner, tree_mask, tree_width):
    rows, width = query_rot.shape
    head_size = width // HEADS
    lanes = 128
    per = lanes // head_size
    groups = width // lanes
    slots, page_len, _ = recv_k.shape
    keys = slots * page_len
    params = pltpu.CompilerParams(vmem_limit_bytes=60 * 1024 * 1024)
    probs_c, probs_d = pl.pallas_call(
        functools.partial(
            _probs_kernel, tree_width=tree_width, head_size=head_size, scale=1.0 / head_size**0.5
        ),
        grid=(groups,),
        in_specs=[
            pl.BlockSpec((rows, lanes), lambda h: (0, h)),
            pl.BlockSpec((slots, page_len, lanes), lambda h: (0, 0, h)),
            pl.BlockSpec((rows, lanes), lambda h: (0, h)),
            pl.BlockSpec((1, keys), lambda h: (0, 0)),
            pl.BlockSpec((rows, rows), lambda h: (0, 0)),
        ],
        out_specs=[
            pl.BlockSpec((None, per, rows, keys), lambda h: (h, 0, 0, 0)),
            pl.BlockSpec((None, per, rows, rows), lambda h: (h, 0, 0, 0)),
        ],
        out_shape=[
            jax.ShapeDtypeStruct((groups, per, rows, keys), jnp.bfloat16),
            jax.ShapeDtypeStruct((groups, per, rows, rows), jnp.bfloat16),
        ],
        compiler_params=params,
    )(query_rot, recv_k, key_rot, key_owner, tree_mask)
    return pl.pallas_call(
        functools.partial(_context_kernel, head_size=head_size),
        grid=(groups,),
        in_specs=[
            pl.BlockSpec((None, per, rows, keys), lambda h: (h, 0, 0, 0)),
            pl.BlockSpec((None, per, rows, rows), lambda h: (h, 0, 0, 0)),
            pl.BlockSpec((slots, page_len, lanes), lambda h: (0, 0, h)),
            pl.BlockSpec((rows, lanes), lambda h: (0, h)),
        ],
        out_specs=pl.BlockSpec((rows, lanes), lambda h: (0, h)),
        out_shape=jax.ShapeDtypeStruct((rows, width), jnp.bfloat16),
        compiler_params=params,
    )(probs_c, probs_d, recv_v, draft_value)


def _ffn_kernel(x_ref, g_ref, win_hbm, wout_hbm, alive_ref, o_ref, win_v, wout_v, sems, *,
                inner, parts):
    step = win_v.shape[0] // parts
    loads = [
        pltpu.make_async_copy(
            win_hbm.at[pl.ds(i * step, step)], win_v.at[pl.ds(i * step, step)], sems.at[i]
        )
        for i in range(parts)
    ]
    load_out = pltpu.make_async_copy(wout_hbm, wout_v, sems.at[parts])
    for load in loads:
        load.start()
    load_out.start()
    x = x_ref[...].astype(jnp.float32)
    mean_value = jnp.mean(x, axis=1, keepdims=True)
    centred = x - mean_value
    variance = jnp.mean(centred * centred, axis=1, keepdims=True)
    normed = (centred * lax.rsqrt(variance + 1e-05) * g_ref[...].astype(jnp.float32)).astype(
        jnp.bfloat16
    )
    both = None
    for i, load in enumerate(loads):
        load.wait()
        part = jnp.dot(
            normed[:, i * step:(i + 1) * step], win_v[pl.ds(i * step, step), :],
            preferred_element_type=jnp.float32,
        )
        both = part if both is None else both + part
    gate = both[:, :inner]
    gelu = 0.5 * gate * (1.0 + lax.erf(gate * (0.5**0.5)))
    middle = (gelu * both[:, inner:]).astype(jnp.bfloat16)
    load_out.wait()
    ffn = jnp.dot(middle, wout_v[...], preferred_element_type=jnp.float32).astype(jnp.bfloat16)
    out = jnp.where(alive_ref[...] > 0, x + ffn.astype(jnp.float32), 0.0)
    o_ref[...] = out.astype(o_ref.dtype)


def feed_forward_out(attended, ln_gain, w_in, w_out, alive):
    rows, width = attended.shape
    inner = w_out.shape[0]
    parts = 4
    whole = lambda shape: pl.BlockSpec(shape, lambda i: (0,) * len(shape))
    return pl.pallas_call(
        functools.partial(_ffn_kernel, inner=inner, parts=parts),
        grid=(1,),
        in_specs=[
            whole((rows, width)),
            whole((1, width)),
            pl.BlockSpec(memory_space=pl.ANY),
            pl.BlockSpec(memory_space=pl.ANY),
            whole((rows, 1)),
        ],
        out_specs=whole((rows, width)),
        out_shape=jax.ShapeDtypeStruct((rows, width), jnp.bfloat16),
        scratch_shapes=[
            pltpu.VMEM(w_in.shape, w_in.dtype),
            pltpu.VMEM(w_out.shape, w_out.dtype),
            pltpu.SemaphoreType.DMA((parts + 1,)),
        ],
        compiler_params=pltpu.CompilerParams(vmem_limit_bytes=62 * 1024 * 1024),
    )(attended, ln_gain.reshape(1, width), w_in, w_out, alive.astype(jnp.int32).reshape(rows, 1))


def local(
    hidden,
    draft_query,
    draft_key,
    draft_value,
    cache_keys,
    cache_values,
    page_target,
    page_slot,
    page_fill,
    tree_parent,
    tree_size,
    accepted_leaf,
    w_attn_out,
    ln_gain,
    w_in,
    w_out,
):
    devices = lax.axis_size("req")
    pages_here, page_len, width = cache_keys.shape
    per_target = max(2, -(-pages_here // devices))
    target = page_target[:, 0]
    onehot = (target[:, None] == jnp.arange(devices, dtype=jnp.int32)[None, :]).astype(jnp.int32)
    within = jnp.sum(jnp.cumsum(onehot, axis=0) * onehot, axis=1) - 1
    dest_slot = target * per_target + within
    slot_count = devices * per_target
    matches = dest_slot[None, :] == jnp.arange(slot_count, dtype=jnp.int32)[:, None]
    filled = jnp.any(matches, axis=1)
    source = jnp.sum(
        jnp.where(matches, jnp.arange(pages_here, dtype=jnp.int32)[None, :], 0), axis=1
    )
    send_fill = jnp.sum(jnp.where(matches, page_fill[None, :], 0), axis=1)
    send_owner = jnp.sum(jnp.where(matches, page_slot[None, :], 0), axis=1)
    send_meta = jnp.stack([send_fill, send_owner], axis=1).reshape(devices, per_target * 2)
    recv_k = lax.all_to_all(
        cache_keys[source].reshape(devices, per_target, page_len, width), "req", 0, 0, tiled=True
    ).reshape(slot_count, page_len, width)
    recv_v = lax.all_to_all(
        cache_values[source].reshape(devices, per_target, page_len, width), "req", 0, 0, tiled=True
    ).reshape(slot_count, page_len, width)
    recv_meta = lax.all_to_all(send_meta, "req", 0, 0, tiled=True).reshape(slot_count, 2)
    recv_fill = recv_meta[:, 0]
    recv_owner = recv_meta[:, 1]
    requests, tree_width = tree_parent.shape
    rows = requests * tree_width
    ancestors = ancestor_closure(tree_parent)
    depth = (jnp.sum(ancestors, axis=2) - 1.0).astype(jnp.int32)
    request_ids = jnp.arange(requests, dtype=jnp.int32)
    cache_len = jnp.sum(
        jnp.where(recv_owner[None, :] == request_ids[:, None], recv_fill[None, :], 0), axis=1
    )
    positions = (cache_len[:, None] + depth).reshape(rows)
    query_rot = rotate_positions(draft_query, positions, HEADS)
    key_rot = rotate_positions(draft_key, positions, HEADS)
    key_owner = jnp.where(
        jnp.arange(page_len, dtype=jnp.int32)[None, :] < recv_fill[:, None], recv_owner[:, None], -1
    ).reshape(1, -1)
    tree_mask = (
        ancestors[:, :, None, :] * jnp.eye(requests, dtype=jnp.float32)[:, None, :, None]
    ).reshape(rows, rows)
    context = attend(query_rot, recv_k, recv_v, key_rot, draft_value, key_owner, tree_mask, tree_width)
    attended = (
        hidden.astype(jnp.float32)
        + jnp.dot(context, w_attn_out, preferred_element_type=jnp.float32)
    ).astype(jnp.bfloat16)
    alive_mask = (jnp.arange(tree_width, dtype=jnp.int32)[None, :] < tree_size[:, None]).reshape(
        rows
    )
    layer_out = feed_forward_out(attended, ln_gain, w_in, w_out, alive_mask)
    leaf_index = jnp.minimum(accepted_leaf, tree_size - 1)
    leaf_onehot = (jnp.arange(tree_width, dtype=jnp.int32)[None, :] == leaf_index[:, None]).astype(
        jnp.float32
    )
    path = jnp.einsum("ri,rij->rj", leaf_onehot, ancestors, precision=lax.Precision.HIGHEST)
    select = (
        path[:, None, :]
        * (depth[:, None, :] == jnp.arange(tree_width, dtype=jnp.int32)[None, :, None]).astype(
            jnp.float32
        )
    ).astype(jnp.bfloat16)
    kept_keys = jnp.einsum(
        "rkj,rjd->rkd",
        select,
        key_rot.reshape(requests, tree_width, width),
        preferred_element_type=jnp.float32,
    )
    kept_values = jnp.einsum(
        "rkj,rjd->rkd",
        select,
        draft_value.reshape(requests, tree_width, width),
        preferred_element_type=jnp.float32,
    )
    return (
        layer_out,
        kept_keys.reshape(rows, width).astype(jnp.bfloat16),
        kept_values.reshape(rows, width).astype(jnp.bfloat16),
    )


def solution(mesh):
    placed = (
        P("req", None),
        P("req", None),
        P("req", None),
        P("req", None),
        P("req", None, None),
        P("req", None, None),
        P("req", None),
        P("req"),
        P("req"),
        P("req", None),
        P("req"),
        P("req"),
        P(),
        P(),
        P(),
        P(),
    )
    return jax.shard_map(
        local,
        mesh=mesh,
        in_specs=placed,
        out_specs=(P("req", None), P("req", None), P("req", None)),
        check_vma=False,
    )
```

```python
import functools

import jax
import jax.numpy as jnp
from jax import lax
from jax.experimental import pallas as pl
from jax.experimental.pallas import tpu as pltpu
from jax.sharding import PartitionSpec as P

HEADS = 16


def ancestor_closure(tree_parent):
    width = tree_parent.shape[1]
    ident = jnp.eye(width, dtype=jnp.float32)
    ancestors = (
        tree_parent[:, :, None] == jnp.arange(width, dtype=jnp.int32)[None, None, :]
    ).astype(jnp.float32) + ident
    for repeat in range((width - 1).bit_length()):
        ancestors = jnp.minimum(
            jnp.einsum("rij,rjk->rik", ancestors, ancestors, precision=lax.Precision.HIGHEST), 1.0
        )
    return ancestors


def rotate_positions(values, positions, heads):
    rows, width = values.shape
    head_size = width // heads
    half = head_size // 2
    inverse = jnp.power(160000.0, -(2.0 * jnp.arange(half, dtype=jnp.float32)) / head_size)
    angle = positions.astype(jnp.float32)[:, None] * inverse[None, :]
    cosine = jnp.cos(angle)[:, None, :]
    sine = jnp.sin(angle)[:, None, :]
    shaped = values.astype(jnp.float32).reshape(rows, heads, head_size)
    first = shaped[..., :half]
    second = shaped[..., half:]
    turned = jnp.concatenate(
        [first * cosine - second * sine, second * cosine + first * sine], axis=-1
    )
    return turned.reshape(rows, width).astype(jnp.bfloat16)


def _probs_kernel(q_ref, kc_ref, kd_ref, kown_ref, tmask_ref, pc_ref, pd_ref, *,
                  tree_width, head_size, scale):
    rows, lanes = q_ref.shape
    q = q_ref[...]
    kc = kc_ref[...].reshape(-1, lanes)
    kd = kd_ref[...]
    lane = lax.broadcasted_iota(jnp.int32, (1, lanes), 1)
    qown = lax.broadcasted_iota(jnp.int32, (rows, 1), 0) // tree_width
    cmask = qown == kown_ref[...]
    tmask = tmask_ref[...] > 0.5
    dims = (((1,), (1,)), ((), ()))
    for part in range(lanes // head_size):
        sel = (lane >= part * head_size) & (lane < (part + 1) * head_size)
        qh = jnp.where(sel, q, jnp.zeros((), q.dtype))
        sc = lax.dot_general(qh, kc, dims, preferred_element_type=jnp.float32) * scale
        sd = lax.dot_general(qh, kd, dims, preferred_element_type=jnp.float32) * scale
        sc = jnp.where(cmask, sc, -1e30)
        sd = jnp.where(tmask, sd, -1e30)
        top = jnp.maximum(jnp.max(sc, axis=1, keepdims=True), jnp.max(sd, axis=1, keepdims=True))
        pc = jnp.exp(sc - top)
        pd = jnp.exp(sd - top)
        inv = 1.0 / (jnp.sum(pc, axis=1, keepdims=True) + jnp.sum(pd, axis=1, keepdims=True))
        pc_ref[part] = (pc * inv).astype(pc_ref.dtype)
        pd_ref[part] = (pd * inv).astype(pd_ref.dtype)


def _context_kernel(pc_ref, pd_ref, vc_ref, vd_ref, o_ref, *, head_size):
    rows, lanes = o_ref.shape
    vc = vc_ref[...].reshape(-1, lanes)
    vd = vd_ref[...]
    lane = lax.broadcasted_iota(jnp.int32, (1, lanes), 1)
    result = None
    for part in range(lanes // head_size):
        ctx = jnp.dot(pc_ref[part], vc, preferred_element_type=jnp.float32)
        ctx = ctx + jnp.dot(pd_ref[part], vd, preferred_element_type=jnp.float32)
        if result is None:
            result = ctx
        else:
            sel = (lane >= part * head_size) & (lane < (part + 1) * head_size)
            result = jnp.where(sel, ctx, result)
    o_ref[...] = result.astype(o_ref.dtype)


def attend(query_rot, recv_k, recv_v, key_rot, draft_value, key_owner, tree_mask, tree_width):
    rows, width = query_rot.shape
    head_size = width // HEADS
    lanes = 128
    per = lanes // head_size
    groups = width // lanes
    slots, page_len, _ = recv_k.shape
    keys = slots * page_len
    params = pltpu.CompilerParams(vmem_limit_bytes=60 * 1024 * 1024)
    probs_c, probs_d = pl.pallas_call(
        functools.partial(
            _probs_kernel, tree_width=tree_width, head_size=head_size, scale=1.0 / head_size**0.5
        ),
        grid=(groups,),
        in_specs=[
            pl.BlockSpec((rows, lanes), lambda h: (0, h)),
            pl.BlockSpec((slots, page_len, lanes), lambda h: (0, 0, h)),
            pl.BlockSpec((rows, lanes), lambda h: (0, h)),
            pl.BlockSpec((1, keys), lambda h: (0, 0)),
            pl.BlockSpec((rows, rows), lambda h: (0, 0)),
        ],
        out_specs=[
            pl.BlockSpec((None, per, rows, keys), lambda h: (h, 0, 0, 0)),
            pl.BlockSpec((None, per, rows, rows), lambda h: (h, 0, 0, 0)),
        ],
        out_shape=[
            jax.ShapeDtypeStruct((groups, per, rows, keys), jnp.bfloat16),
            jax.ShapeDtypeStruct((groups, per, rows, rows), jnp.bfloat16),
        ],
        compiler_params=params,
    )(query_rot, recv_k, key_rot, key_owner, tree_mask)
    return pl.pallas_call(
        functools.partial(_context_kernel, head_size=head_size),
        grid=(groups,),
        in_specs=[
            pl.BlockSpec((None, per, rows, keys), lambda h: (h, 0, 0, 0)),
            pl.BlockSpec((None, per, rows, rows), lambda h: (h, 0, 0, 0)),
            pl.BlockSpec((slots, page_len, lanes), lambda h: (0, 0, h)),
            pl.BlockSpec((rows, lanes), lambda h: (0, h)),
        ],
        out_specs=pl.BlockSpec((rows, lanes), lambda h: (0, h)),
        out_shape=jax.ShapeDtypeStruct((rows, width), jnp.bfloat16),
        compiler_params=params,
    )(probs_c, probs_d, recv_v, draft_value)


def _ffn_kernel(h_ref, c_ref, wo_hbm, g_ref, win_hbm, wout_hbm, alive_ref, o_ref, wo_v, win_v,
                wout_v, sems, *, inner, parts):
    step = win_v.shape[0] // parts
    load_proj = pltpu.make_async_copy(wo_hbm, wo_v, sems.at[parts + 1])
    load_proj.start()
    loads = [
        pltpu.make_async_copy(
            win_hbm.at[pl.ds(i * step, step)], win_v.at[pl.ds(i * step, step)], sems.at[i]
        )
        for i in range(parts)
    ]
    load_out = pltpu.make_async_copy(wout_hbm, wout_v, sems.at[parts])
    for load in loads:
        load.start()
    load_out.start()
    load_proj.wait()
    attended = h_ref[...].astype(jnp.float32) + jnp.dot(
        c_ref[...], wo_v[...], preferred_element_type=jnp.float32
    )
    x = attended.astype(jnp.bfloat16).astype(jnp.float32)
    mean_value = jnp.mean(x, axis=1, keepdims=True)
    centred = x - mean_value
    variance = jnp.mean(centred * centred, axis=1, keepdims=True)
    normed = (centred * lax.rsqrt(variance + 1e-05) * g_ref[...].astype(jnp.float32)).astype(
        jnp.bfloat16
    )
    both = None
    for i, load in enumerate(loads):
        load.wait()
        part = jnp.dot(
            normed[:, i * step:(i + 1) * step], win_v[pl.ds(i * step, step), :],
            preferred_element_type=jnp.float32,
        )
        both = part if both is None else both + part
    gate = both[:, :inner]
    gelu = 0.5 * gate * (1.0 + lax.erf(gate * (0.5**0.5)))
    middle = (gelu * both[:, inner:]).astype(jnp.bfloat16)
    load_out.wait()
    ffn = jnp.dot(middle, wout_v[...], preferred_element_type=jnp.float32).astype(jnp.bfloat16)
    out = jnp.where(alive_ref[...] > 0, x + ffn.astype(jnp.float32), 0.0)
    o_ref[...] = out.astype(o_ref.dtype)


def feed_forward_out(hidden, context, w_attn_out, ln_gain, w_in, w_out, alive):
    rows, width = hidden.shape
    inner = w_out.shape[0]
    parts = 4
    whole = lambda shape: pl.BlockSpec(shape, lambda i: (0,) * len(shape))
    return pl.pallas_call(
        functools.partial(_ffn_kernel, inner=inner, parts=parts),
        grid=(1,),
        in_specs=[
            whole((rows, width)),
            whole((rows, width)),
            pl.BlockSpec(memory_space=pl.ANY),
            whole((1, width)),
            pl.BlockSpec(memory_space=pl.ANY),
            pl.BlockSpec(memory_space=pl.ANY),
            whole((rows, 1)),
        ],
        out_specs=whole((rows, width)),
        out_shape=jax.ShapeDtypeStruct((rows, width), jnp.bfloat16),
        scratch_shapes=[
            pltpu.VMEM(w_attn_out.shape, w_attn_out.dtype),
            pltpu.VMEM(w_in.shape, w_in.dtype),
            pltpu.VMEM(w_out.shape, w_out.dtype),
            pltpu.SemaphoreType.DMA((parts + 2,)),
        ],
        compiler_params=pltpu.CompilerParams(vmem_limit_bytes=62 * 1024 * 1024),
    )(
        hidden, context, w_attn_out, ln_gain.reshape(1, width), w_in, w_out,
        alive.astype(jnp.int32).reshape(rows, 1),
    )


def local(
    hidden,
    draft_query,
    draft_key,
    draft_value,
    cache_keys,
    cache_values,
    page_target,
    page_slot,
    page_fill,
    tree_parent,
    tree_size,
    accepted_leaf,
    w_attn_out,
    ln_gain,
    w_in,
    w_out,
):
    devices = lax.axis_size("req")
    pages_here, page_len, width = cache_keys.shape
    per_target = max(2, -(-pages_here // devices))
    target = page_target[:, 0]
    onehot = (target[:, None] == jnp.arange(devices, dtype=jnp.int32)[None, :]).astype(jnp.int32)
    within = jnp.sum(jnp.cumsum(onehot, axis=0) * onehot, axis=1) - 1
    dest_slot = target * per_target + within
    slot_count = devices * per_target
    matches = dest_slot[None, :] == jnp.arange(slot_count, dtype=jnp.int32)[:, None]
    filled = jnp.any(matches, axis=1)
    source = jnp.sum(
        jnp.where(matches, jnp.arange(pages_here, dtype=jnp.int32)[None, :], 0), axis=1
    )
    send_fill = jnp.sum(jnp.where(matches, page_fill[None, :], 0), axis=1)
    send_owner = jnp.sum(jnp.where(matches, page_slot[None, :], 0), axis=1)
    send_meta = jnp.stack([send_fill, send_owner], axis=1).reshape(devices, per_target * 2)
    recv_k = lax.all_to_all(
        cache_keys[source].reshape(devices, per_target, page_len, width), "req", 0, 0, tiled=True
    ).reshape(slot_count, page_len, width)
    recv_v = lax.all_to_all(
        cache_values[source].reshape(devices, per_target, page_len, width), "req", 0, 0, tiled=True
    ).reshape(slot_count, page_len, width)
    recv_meta = lax.all_to_all(send_meta, "req", 0, 0, tiled=True).reshape(slot_count, 2)
    recv_fill = recv_meta[:, 0]
    recv_owner = recv_meta[:, 1]
    requests, tree_width = tree_parent.shape
    rows = requests * tree_width
    ancestors = ancestor_closure(tree_parent)
    depth = (jnp.sum(ancestors, axis=2) - 1.0).astype(jnp.int32)
    request_ids = jnp.arange(requests, dtype=jnp.int32)
    cache_len = jnp.sum(
        jnp.where(recv_owner[None, :] == request_ids[:, None], recv_fill[None, :], 0), axis=1
    )
    positions = (cache_len[:, None] + depth).reshape(rows)
    query_rot = rotate_positions(draft_query, positions, HEADS)
    key_rot = rotate_positions(draft_key, positions, HEADS)
    key_owner = jnp.where(
        jnp.arange(page_len, dtype=jnp.int32)[None, :] < recv_fill[:, None], recv_owner[:, None], -1
    ).reshape(1, -1)
    tree_mask = (
        ancestors[:, :, None, :] * jnp.eye(requests, dtype=jnp.float32)[:, None, :, None]
    ).reshape(rows, rows)
    context = attend(query_rot, recv_k, recv_v, key_rot, draft_value, key_owner, tree_mask, tree_width)
    alive_mask = (jnp.arange(tree_width, dtype=jnp.int32)[None, :] < tree_size[:, None]).reshape(
        rows
    )
    layer_out = feed_forward_out(hidden, context, w_attn_out, ln_gain, w_in, w_out, alive_mask)
    leaf_index = jnp.minimum(accepted_leaf, tree_size - 1)
    leaf_onehot = (jnp.arange(tree_width, dtype=jnp.int32)[None, :] == leaf_index[:, None]).astype(
        jnp.float32
    )
    path = jnp.einsum("ri,rij->rj", leaf_onehot, ancestors, precision=lax.Precision.HIGHEST)
    select = (
        path[:, None, :]
        * (depth[:, None, :] == jnp.arange(tree_width, dtype=jnp.int32)[None, :, None]).astype(
            jnp.float32
        )
    ).astype(jnp.bfloat16)
    kept_keys = jnp.einsum(
        "rkj,rjd->rkd",
        select,
        key_rot.reshape(requests, tree_width, width),
        preferred_element_type=jnp.float32,
    )
    kept_values = jnp.einsum(
        "rkj,rjd->rkd",
        select,
        draft_value.reshape(requests, tree_width, width),
        preferred_element_type=jnp.float32,
    )
    return (
        layer_out,
        kept_keys.reshape(rows, width).astype(jnp.bfloat16),
        kept_values.reshape(rows, width).astype(jnp.bfloat16),
    )


def solution(mesh):
    placed = (
        P("req", None),
        P("req", None),
        P("req", None),
        P("req", None),
        P("req", None, None),
        P("req", None, None),
        P("req", None),
        P("req"),
        P("req"),
        P("req", None),
        P("req"),
        P("req"),
        P(),
        P(),
        P(),
        P(),
    )
    return jax.shard_map(
        local,
        mesh=mesh,
        in_specs=placed,
        out_specs=(P("req", None), P("req", None), P("req", None)),
        check_vma=False,
    )
```

```python
import functools

import jax
import jax.numpy as jnp
from jax import lax
from jax.experimental import pallas as pl
from jax.experimental.pallas import tpu as pltpu
from jax.sharding import PartitionSpec as P

HEADS = 16


def ancestor_closure(tree_parent):
    width = tree_parent.shape[1]
    ident = jnp.eye(width, dtype=jnp.float32)
    ancestors = (
        tree_parent[:, :, None] == jnp.arange(width, dtype=jnp.int32)[None, None, :]
    ).astype(jnp.float32) + ident
    for repeat in range((width - 1).bit_length()):
        ancestors = jnp.minimum(
            jnp.einsum("rij,rjk->rik", ancestors, ancestors, precision=lax.Precision.HIGHEST), 1.0
        )
    return ancestors


def rotate_positions(values, positions, heads):
    rows, width = values.shape
    head_size = width // heads
    half = head_size // 2
    inverse = jnp.power(160000.0, -(2.0 * jnp.arange(half, dtype=jnp.float32)) / head_size)
    angle = positions.astype(jnp.float32)[:, None] * inverse[None, :]
    cosine = jnp.cos(angle)[:, None, :]
    sine = jnp.sin(angle)[:, None, :]
    shaped = values.astype(jnp.float32).reshape(rows, heads, head_size)
    first = shaped[..., :half]
    second = shaped[..., half:]
    turned = jnp.concatenate(
        [first * cosine - second * sine, second * cosine + first * sine], axis=-1
    )
    return turned.reshape(rows, width).astype(jnp.bfloat16)


def _probs_kernel(q_ref, kc_ref, kd_ref, vd_ref, kown_ref, tmask_ref, pc_ref, cd_ref, *,
                  tree_width, head_size, scale):
    rows, lanes = q_ref.shape
    q = q_ref[...]
    kc = kc_ref[...].reshape(-1, lanes)
    kd = kd_ref[...]
    lane = lax.broadcasted_iota(jnp.int32, (1, lanes), 1)
    qown = lax.broadcasted_iota(jnp.int32, (rows, 1), 0) // tree_width
    cmask = qown == kown_ref[...]
    tmask = tmask_ref[...] > 0.5
    vd = vd_ref[...]
    dims = (((1,), (1,)), ((), ()))
    draft = None
    for part in range(lanes // head_size):
        sel = (lane >= part * head_size) & (lane < (part + 1) * head_size)
        qh = jnp.where(sel, q, jnp.zeros((), q.dtype))
        sc = lax.dot_general(qh, kc, dims, preferred_element_type=jnp.float32) * scale
        sd = lax.dot_general(qh, kd, dims, preferred_element_type=jnp.float32) * scale
        sc = jnp.where(cmask, sc, -1e30)
        sd = jnp.where(tmask, sd, -1e30)
        top = jnp.maximum(jnp.max(sc, axis=1, keepdims=True), jnp.max(sd, axis=1, keepdims=True))
        pc = jnp.exp(sc - top)
        pd = jnp.exp(sd - top)
        inv = 1.0 / (jnp.sum(pc, axis=1, keepdims=True) + jnp.sum(pd, axis=1, keepdims=True))
        pc_ref[part] = (pc * inv).astype(pc_ref.dtype)
        ctx = jnp.dot((pd * inv).astype(jnp.bfloat16), vd, preferred_element_type=jnp.float32)
        draft = ctx if draft is None else jnp.where(sel, ctx, draft)
    cd_ref[...] = draft


def _context_kernel(pc_ref, cd_ref, vc_ref, o_ref, *, head_size):
    rows, lanes = o_ref.shape
    vc = vc_ref[...].reshape(-1, lanes)
    draft = cd_ref[...]
    lane = lax.broadcasted_iota(jnp.int32, (1, lanes), 1)
    result = None
    for part in range(lanes // head_size):
        ctx = jnp.dot(pc_ref[part], vc, preferred_element_type=jnp.float32)
        ctx = ctx + draft
        if result is None:
            result = ctx
        else:
            sel = (lane >= part * head_size) & (lane < (part + 1) * head_size)
            result = jnp.where(sel, ctx, result)
    o_ref[...] = result.astype(o_ref.dtype)


def attend(query_rot, recv_k, recv_v, key_rot, draft_value, key_owner, tree_mask, tree_width):
    rows, width = query_rot.shape
    head_size = width // HEADS
    lanes = 128
    per = lanes // head_size
    groups = width // lanes
    slots, page_len, _ = recv_k.shape
    keys = slots * page_len
    params = pltpu.CompilerParams(vmem_limit_bytes=60 * 1024 * 1024)
    probs_c, draft_ctx = pl.pallas_call(
        functools.partial(
            _probs_kernel, tree_width=tree_width, head_size=head_size, scale=1.0 / head_size**0.5
        ),
        grid=(groups,),
        in_specs=[
            pl.BlockSpec((rows, lanes), lambda h: (0, h)),
            pl.BlockSpec((slots, page_len, lanes), lambda h: (0, 0, h)),
            pl.BlockSpec((rows, lanes), lambda h: (0, h)),
            pl.BlockSpec((rows, lanes), lambda h: (0, h)),
            pl.BlockSpec((1, keys), lambda h: (0, 0)),
            pl.BlockSpec((rows, rows), lambda h: (0, 0)),
        ],
        out_specs=[
            pl.BlockSpec((None, per, rows, keys), lambda h: (h, 0, 0, 0)),
            pl.BlockSpec((rows, lanes), lambda h: (0, h)),
        ],
        out_shape=[
            jax.ShapeDtypeStruct((groups, per, rows, keys), jnp.bfloat16),
            jax.ShapeDtypeStruct((rows, width), jnp.float32),
        ],
        compiler_params=params,
    )(query_rot, recv_k, key_rot, draft_value, key_owner, tree_mask)
    return pl.pallas_call(
        functools.partial(_context_kernel, head_size=head_size),
        grid=(groups,),
        in_specs=[
            pl.BlockSpec((None, per, rows, keys), lambda h: (h, 0, 0, 0)),
            pl.BlockSpec((rows, lanes), lambda h: (0, h)),
            pl.BlockSpec((slots, page_len, lanes), lambda h: (0, 0, h)),
        ],
        out_specs=pl.BlockSpec((rows, lanes), lambda h: (0, h)),
        out_shape=jax.ShapeDtypeStruct((rows, width), jnp.bfloat16),
        compiler_params=params,
    )(probs_c, draft_ctx, recv_v)


def _ffn_kernel(h_ref, c_ref, wo_hbm, g_ref, win_hbm, wout_hbm, alive_ref, o_ref, wo_v, win_v,
                wout_v, sems, *, inner, parts):
    step = win_v.shape[0] // parts
    load_proj = pltpu.make_async_copy(wo_hbm, wo_v, sems.at[parts + 1])
    load_proj.start()
    loads = [
        pltpu.make_async_copy(
            win_hbm.at[pl.ds(i * step, step)], win_v.at[pl.ds(i * step, step)], sems.at[i]
        )
        for i in range(parts)
    ]
    load_out = pltpu.make_async_copy(wout_hbm, wout_v, sems.at[parts])
    for load in loads:
        load.start()
    load_out.start()
    load_proj.wait()
    attended = h_ref[...].astype(jnp.float32) + jnp.dot(
        c_ref[...], wo_v[...], preferred_element_type=jnp.float32
    )
    x = attended.astype(jnp.bfloat16).astype(jnp.float32)
    mean_value = jnp.mean(x, axis=1, keepdims=True)
    centred = x - mean_value
    variance = jnp.mean(centred * centred, axis=1, keepdims=True)
    normed = (centred * lax.rsqrt(variance + 1e-05) * g_ref[...].astype(jnp.float32)).astype(
        jnp.bfloat16
    )
    both = None
    for i, load in enumerate(loads):
        load.wait()
        part = jnp.dot(
            normed[:, i * step:(i + 1) * step], win_v[pl.ds(i * step, step), :],
            preferred_element_type=jnp.float32,
        )
        both = part if both is None else both + part
    gate = both[:, :inner]
    gelu = 0.5 * gate * (1.0 + lax.erf(gate * (0.5**0.5)))
    middle = (gelu * both[:, inner:]).astype(jnp.bfloat16)
    load_out.wait()
    ffn = jnp.dot(middle, wout_v[...], preferred_element_type=jnp.float32).astype(jnp.bfloat16)
    out = jnp.where(alive_ref[...] > 0, x + ffn.astype(jnp.float32), 0.0)
    o_ref[...] = out.astype(o_ref.dtype)


def feed_forward_out(hidden, context, w_attn_out, ln_gain, w_in, w_out, alive):
    rows, width = hidden.shape
    inner = w_out.shape[0]
    parts = 4
    whole = lambda shape: pl.BlockSpec(shape, lambda i: (0,) * len(shape))
    return pl.pallas_call(
        functools.partial(_ffn_kernel, inner=inner, parts=parts),
        grid=(1,),
        in_specs=[
            whole((rows, width)),
            whole((rows, width)),
            pl.BlockSpec(memory_space=pl.ANY),
            whole((1, width)),
            pl.BlockSpec(memory_space=pl.ANY),
            pl.BlockSpec(memory_space=pl.ANY),
            whole((rows, 1)),
        ],
        out_specs=whole((rows, width)),
        out_shape=jax.ShapeDtypeStruct((rows, width), jnp.bfloat16),
        scratch_shapes=[
            pltpu.VMEM(w_attn_out.shape, w_attn_out.dtype),
            pltpu.VMEM(w_in.shape, w_in.dtype),
            pltpu.VMEM(w_out.shape, w_out.dtype),
            pltpu.SemaphoreType.DMA((parts + 2,)),
        ],
        compiler_params=pltpu.CompilerParams(vmem_limit_bytes=62 * 1024 * 1024),
    )(
        hidden, context, w_attn_out, ln_gain.reshape(1, width), w_in, w_out,
        alive.astype(jnp.int32).reshape(rows, 1),
    )


def local(
    hidden,
    draft_query,
    draft_key,
    draft_value,
    cache_keys,
    cache_values,
    page_target,
    page_slot,
    page_fill,
    tree_parent,
    tree_size,
    accepted_leaf,
    w_attn_out,
    ln_gain,
    w_in,
    w_out,
):
    devices = lax.axis_size("req")
    pages_here, page_len, width = cache_keys.shape
    per_target = max(2, -(-pages_here // devices))
    target = page_target[:, 0]
    onehot = (target[:, None] == jnp.arange(devices, dtype=jnp.int32)[None, :]).astype(jnp.int32)
    within = jnp.sum(jnp.cumsum(onehot, axis=0) * onehot, axis=1) - 1
    dest_slot = target * per_target + within
    slot_count = devices * per_target
    matches = dest_slot[None, :] == jnp.arange(slot_count, dtype=jnp.int32)[:, None]
    filled = jnp.any(matches, axis=1)
    source = jnp.sum(
        jnp.where(matches, jnp.arange(pages_here, dtype=jnp.int32)[None, :], 0), axis=1
    )
    send_fill = jnp.sum(jnp.where(matches, page_fill[None, :], 0), axis=1)
    send_owner = jnp.sum(jnp.where(matches, page_slot[None, :], 0), axis=1)
    send_meta = jnp.stack([send_fill, send_owner], axis=1).reshape(devices, per_target * 2)
    recv_k = lax.all_to_all(
        cache_keys[source].reshape(devices, per_target, page_len, width), "req", 0, 0, tiled=True
    ).reshape(slot_count, page_len, width)
    recv_v = lax.all_to_all(
        cache_values[source].reshape(devices, per_target, page_len, width), "req", 0, 0, tiled=True
    ).reshape(slot_count, page_len, width)
    recv_meta = lax.all_to_all(send_meta, "req", 0, 0, tiled=True).reshape(slot_count, 2)
    recv_fill = recv_meta[:, 0]
    recv_owner = recv_meta[:, 1]
    requests, tree_width = tree_parent.shape
    rows = requests * tree_width
    ancestors = ancestor_closure(tree_parent)
    depth = (jnp.sum(ancestors, axis=2) - 1.0).astype(jnp.int32)
    request_ids = jnp.arange(requests, dtype=jnp.int32)
    cache_len = jnp.sum(
        jnp.where(recv_owner[None, :] == request_ids[:, None], recv_fill[None, :], 0), axis=1
    )
    positions = (cache_len[:, None] + depth).reshape(rows)
    query_rot = rotate_positions(draft_query, positions, HEADS)
    key_rot = rotate_positions(draft_key, positions, HEADS)
    key_owner = jnp.where(
        jnp.arange(page_len, dtype=jnp.int32)[None, :] < recv_fill[:, None], recv_owner[:, None], -1
    ).reshape(1, -1)
    tree_mask = (
        ancestors[:, :, None, :] * jnp.eye(requests, dtype=jnp.float32)[:, None, :, None]
    ).reshape(rows, rows)
    context = attend(query_rot, recv_k, recv_v, key_rot, draft_value, key_owner, tree_mask, tree_width)
    alive_mask = (jnp.arange(tree_width, dtype=jnp.int32)[None, :] < tree_size[:, None]).reshape(
        rows
    )
    layer_out = feed_forward_out(hidden, context, w_attn_out, ln_gain, w_in, w_out, alive_mask)
    leaf_index = jnp.minimum(accepted_leaf, tree_size - 1)
    leaf_onehot = (jnp.arange(tree_width, dtype=jnp.int32)[None, :] == leaf_index[:, None]).astype(
        jnp.float32
    )
    path = jnp.einsum("ri,rij->rj", leaf_onehot, ancestors, precision=lax.Precision.HIGHEST)
    select = (
        path[:, None, :]
        * (depth[:, None, :] == jnp.arange(tree_width, dtype=jnp.int32)[None, :, None]).astype(
            jnp.float32
        )
    ).astype(jnp.bfloat16)
    kept_keys = jnp.einsum(
        "rkj,rjd->rkd",
        select,
        key_rot.reshape(requests, tree_width, width),
        preferred_element_type=jnp.float32,
    )
    kept_values = jnp.einsum(
        "rkj,rjd->rkd",
        select,
        draft_value.reshape(requests, tree_width, width),
        preferred_element_type=jnp.float32,
    )
    return (
        layer_out,
        kept_keys.reshape(rows, width).astype(jnp.bfloat16),
        kept_values.reshape(rows, width).astype(jnp.bfloat16),
    )


def solution(mesh):
    placed = (
        P("req", None),
        P("req", None),
        P("req", None),
        P("req", None),
        P("req", None, None),
        P("req", None, None),
        P("req", None),
        P("req"),
        P("req"),
        P("req", None),
        P("req"),
        P("req"),
        P(),
        P(),
        P(),
        P(),
    )
    return jax.shard_map(
        local,
        mesh=mesh,
        in_specs=placed,
        out_specs=(P("req", None), P("req", None), P("req", None)),
        check_vma=False,
    )
```

```python
import functools

import jax
import jax.numpy as jnp
from jax import lax
from jax.experimental import pallas as pl
from jax.experimental.pallas import tpu as pltpu
from jax.sharding import PartitionSpec as P

HEADS = 16


def ancestor_closure(tree_parent):
    width = tree_parent.shape[1]
    ident = jnp.eye(width, dtype=jnp.float32)
    ancestors = (
        tree_parent[:, :, None] == jnp.arange(width, dtype=jnp.int32)[None, None, :]
    ).astype(jnp.float32) + ident
    for repeat in range((width - 1).bit_length()):
        ancestors = jnp.minimum(
            jnp.einsum("rij,rjk->rik", ancestors, ancestors, precision=lax.Precision.HIGHEST), 1.0
        )
    return ancestors


def rotate_positions(values, positions, heads):
    rows, width = values.shape
    head_size = width // heads
    half = head_size // 2
    inverse = jnp.power(160000.0, -(2.0 * jnp.arange(half, dtype=jnp.float32)) / head_size)
    angle = positions.astype(jnp.float32)[:, None] * inverse[None, :]
    cosine = jnp.cos(angle)[:, None, :]
    sine = jnp.sin(angle)[:, None, :]
    shaped = values.astype(jnp.float32).reshape(rows, heads, head_size)
    first = shaped[..., :half]
    second = shaped[..., half:]
    turned = jnp.concatenate(
        [first * cosine - second * sine, second * cosine + first * sine], axis=-1
    )
    return turned.reshape(rows, width).astype(jnp.bfloat16)


def _probs_kernel(q_ref, kc_ref, kd_ref, vd_ref, kown_ref, tmask_ref, pc_ref, cd_ref, *,
                  tree_width, head_size, scale):
    rows, lanes = q_ref.shape
    q = q_ref[...]
    kc = kc_ref[...].reshape(-1, lanes)
    kd = kd_ref[...]
    lane = lax.broadcasted_iota(jnp.int32, (1, lanes), 1)
    qown = lax.broadcasted_iota(jnp.int32, (rows, 1), 0) // tree_width
    cmask = qown == kown_ref[...]
    tmask = tmask_ref[...] > 0.5
    vd = vd_ref[...]
    dims = (((1,), (1,)), ((), ()))
    draft = None
    for part in range(lanes // head_size):
        sel = (lane >= part * head_size) & (lane < (part + 1) * head_size)
        qh = jnp.where(sel, q, jnp.zeros((), q.dtype))
        sc = lax.dot_general(qh, kc, dims, preferred_element_type=jnp.float32) * scale
        sd = lax.dot_general(qh, kd, dims, preferred_element_type=jnp.float32) * scale
        sc = jnp.where(cmask, sc, -1e30)
        sd = jnp.where(tmask, sd, -1e30)
        top = jnp.maximum(jnp.max(sc, axis=1, keepdims=True), jnp.max(sd, axis=1, keepdims=True))
        pc = jnp.exp(sc - top)
        pd = jnp.exp(sd - top)
        inv = 1.0 / (jnp.sum(pc, axis=1, keepdims=True) + jnp.sum(pd, axis=1, keepdims=True))
        pc_ref[part] = (pc * inv).astype(pc_ref.dtype)
        ctx = jnp.dot((pd * inv).astype(jnp.bfloat16), vd, preferred_element_type=jnp.float32)
        draft = ctx if draft is None else jnp.where(sel, ctx, draft)
    cd_ref[...] = draft


def _context_kernel(pc_ref, cd_ref, vc_ref, o_ref, *, head_size):
    rows, lanes = o_ref.shape
    part = pl.program_id(0) % (lanes // head_size)
    vc = vc_ref[...].reshape(-1, lanes)
    ctx = jnp.dot(pc_ref[...], vc, preferred_element_type=jnp.float32) + cd_ref[...]
    lane = lax.broadcasted_iota(jnp.int32, (1, lanes), 1)

    @pl.when(part == 0)
    def _():
        o_ref[...] = ctx.astype(o_ref.dtype)

    @pl.when(part > 0)
    def _():
        sel = lane >= part * head_size
        o_ref[...] = jnp.where(sel, ctx.astype(o_ref.dtype), o_ref[...])


def attend(query_rot, recv_k, recv_v, key_rot, draft_value, key_owner, tree_mask, tree_width):
    rows, width = query_rot.shape
    head_size = width // HEADS
    lanes = 128
    per = lanes // head_size
    groups = width // lanes
    slots, page_len, _ = recv_k.shape
    keys = slots * page_len
    params = pltpu.CompilerParams(vmem_limit_bytes=60 * 1024 * 1024)
    probs_c, draft_ctx = pl.pallas_call(
        functools.partial(
            _probs_kernel, tree_width=tree_width, head_size=head_size, scale=1.0 / head_size**0.5
        ),
        grid=(groups,),
        in_specs=[
            pl.BlockSpec((rows, lanes), lambda h: (0, h)),
            pl.BlockSpec((slots, page_len, lanes), lambda h: (0, 0, h)),
            pl.BlockSpec((rows, lanes), lambda h: (0, h)),
            pl.BlockSpec((rows, lanes), lambda h: (0, h)),
            pl.BlockSpec((1, keys), lambda h: (0, 0)),
            pl.BlockSpec((rows, rows), lambda h: (0, 0)),
        ],
        out_specs=[
            pl.BlockSpec((None, per, rows, keys), lambda h: (h, 0, 0, 0)),
            pl.BlockSpec((rows, lanes), lambda h: (0, h)),
        ],
        out_shape=[
            jax.ShapeDtypeStruct((groups, per, rows, keys), jnp.bfloat16),
            jax.ShapeDtypeStruct((rows, width), jnp.float32),
        ],
        compiler_params=params,
    )(query_rot, recv_k, key_rot, draft_value, key_owner, tree_mask)
    return pl.pallas_call(
        functools.partial(_context_kernel, head_size=head_size),
        grid=(groups * per,),
        in_specs=[
            pl.BlockSpec((None, None, rows, keys), lambda h: (h // per, h % per, 0, 0)),
            pl.BlockSpec((rows, lanes), lambda h: (0, h // per)),
            pl.BlockSpec((slots, page_len, lanes), lambda h: (0, 0, h // per)),
        ],
        out_specs=pl.BlockSpec((rows, lanes), lambda h: (0, h // per)),
        out_shape=jax.ShapeDtypeStruct((rows, width), jnp.bfloat16),
        compiler_params=params,
    )(probs_c, draft_ctx, recv_v)


def _ffn_kernel(h_ref, c_ref, wo_hbm, g_ref, win_hbm, wout_hbm, alive_ref, o_ref, wo_v, win_v,
                wout_v, sems, *, inner, parts):
    step = win_v.shape[0] // parts
    load_proj = pltpu.make_async_copy(wo_hbm, wo_v, sems.at[parts + 1])
    load_proj.start()
    loads = [
        pltpu.make_async_copy(
            win_hbm.at[pl.ds(i * step, step)], win_v.at[pl.ds(i * step, step)], sems.at[i]
        )
        for i in range(parts)
    ]
    load_out = pltpu.make_async_copy(wout_hbm, wout_v, sems.at[parts])
    for load in loads:
        load.start()
    load_out.start()
    load_proj.wait()
    attended = h_ref[...].astype(jnp.float32) + jnp.dot(
        c_ref[...], wo_v[...], preferred_element_type=jnp.float32
    )
    x = attended.astype(jnp.bfloat16).astype(jnp.float32)
    mean_value = jnp.mean(x, axis=1, keepdims=True)
    centred = x - mean_value
    variance = jnp.mean(centred * centred, axis=1, keepdims=True)
    normed = (centred * lax.rsqrt(variance + 1e-05) * g_ref[...].astype(jnp.float32)).astype(
        jnp.bfloat16
    )
    both = None
    for i, load in enumerate(loads):
        load.wait()
        part = jnp.dot(
            normed[:, i * step:(i + 1) * step], win_v[pl.ds(i * step, step), :],
            preferred_element_type=jnp.float32,
        )
        both = part if both is None else both + part
    gate = both[:, :inner]
    gelu = 0.5 * gate * (1.0 + lax.erf(gate * (0.5**0.5)))
    middle = (gelu * both[:, inner:]).astype(jnp.bfloat16)
    load_out.wait()
    ffn = jnp.dot(middle, wout_v[...], preferred_element_type=jnp.float32).astype(jnp.bfloat16)
    out = jnp.where(alive_ref[...] > 0, x + ffn.astype(jnp.float32), 0.0)
    o_ref[...] = out.astype(o_ref.dtype)


def feed_forward_out(hidden, context, w_attn_out, ln_gain, w_in, w_out, alive):
    rows, width = hidden.shape
    inner = w_out.shape[0]
    parts = 4
    whole = lambda shape: pl.BlockSpec(shape, lambda i: (0,) * len(shape))
    return pl.pallas_call(
        functools.partial(_ffn_kernel, inner=inner, parts=parts),
        grid=(1,),
        in_specs=[
            whole((rows, width)),
            whole((rows, width)),
            pl.BlockSpec(memory_space=pl.ANY),
            whole((1, width)),
            pl.BlockSpec(memory_space=pl.ANY),
            pl.BlockSpec(memory_space=pl.ANY),
            whole((rows, 1)),
        ],
        out_specs=whole((rows, width)),
        out_shape=jax.ShapeDtypeStruct((rows, width), jnp.bfloat16),
        scratch_shapes=[
            pltpu.VMEM(w_attn_out.shape, w_attn_out.dtype),
            pltpu.VMEM(w_in.shape, w_in.dtype),
            pltpu.VMEM(w_out.shape, w_out.dtype),
            pltpu.SemaphoreType.DMA((parts + 2,)),
        ],
        compiler_params=pltpu.CompilerParams(vmem_limit_bytes=62 * 1024 * 1024),
    )(
        hidden, context, w_attn_out, ln_gain.reshape(1, width), w_in, w_out,
        alive.astype(jnp.int32).reshape(rows, 1),
    )


def local(
    hidden,
    draft_query,
    draft_key,
    draft_value,
    cache_keys,
    cache_values,
    page_target,
    page_slot,
    page_fill,
    tree_parent,
    tree_size,
    accepted_leaf,
    w_attn_out,
    ln_gain,
    w_in,
    w_out,
):
    devices = lax.axis_size("req")
    pages_here, page_len, width = cache_keys.shape
    per_target = max(2, -(-pages_here // devices))
    target = page_target[:, 0]
    onehot = (target[:, None] == jnp.arange(devices, dtype=jnp.int32)[None, :]).astype(jnp.int32)
    within = jnp.sum(jnp.cumsum(onehot, axis=0) * onehot, axis=1) - 1
    dest_slot = target * per_target + within
    slot_count = devices * per_target
    matches = dest_slot[None, :] == jnp.arange(slot_count, dtype=jnp.int32)[:, None]
    filled = jnp.any(matches, axis=1)
    source = jnp.sum(
        jnp.where(matches, jnp.arange(pages_here, dtype=jnp.int32)[None, :], 0), axis=1
    )
    send_fill = jnp.sum(jnp.where(matches, page_fill[None, :], 0), axis=1)
    send_owner = jnp.sum(jnp.where(matches, page_slot[None, :], 0), axis=1)
    send_meta = jnp.stack([send_fill, send_owner], axis=1).reshape(devices, per_target * 2)
    recv_k = lax.all_to_all(
        cache_keys[source].reshape(devices, per_target, page_len, width), "req", 0, 0, tiled=True
    ).reshape(slot_count, page_len, width)
    recv_v = lax.all_to_all(
        cache_values[source].reshape(devices, per_target, page_len, width), "req", 0, 0, tiled=True
    ).reshape(slot_count, page_len, width)
    recv_meta = lax.all_to_all(send_meta, "req", 0, 0, tiled=True).reshape(slot_count, 2)
    recv_fill = recv_meta[:, 0]
    recv_owner = recv_meta[:, 1]
    requests, tree_width = tree_parent.shape
    rows = requests * tree_width
    ancestors = ancestor_closure(tree_parent)
    depth = (jnp.sum(ancestors, axis=2) - 1.0).astype(jnp.int32)
    request_ids = jnp.arange(requests, dtype=jnp.int32)
    cache_len = jnp.sum(
        jnp.where(recv_owner[None, :] == request_ids[:, None], recv_fill[None, :], 0), axis=1
    )
    positions = (cache_len[:, None] + depth).reshape(rows)
    query_rot = rotate_positions(draft_query, positions, HEADS)
    key_rot = rotate_positions(draft_key, positions, HEADS)
    key_owner = jnp.where(
        jnp.arange(page_len, dtype=jnp.int32)[None, :] < recv_fill[:, None], recv_owner[:, None], -1
    ).reshape(1, -1)
    tree_mask = (
        ancestors[:, :, None, :] * jnp.eye(requests, dtype=jnp.float32)[:, None, :, None]
    ).reshape(rows, rows)
    context = attend(query_rot, recv_k, recv_v, key_rot, draft_value, key_owner, tree_mask, tree_width)
    alive_mask = (jnp.arange(tree_width, dtype=jnp.int32)[None, :] < tree_size[:, None]).reshape(
        rows
    )
    layer_out = feed_forward_out(hidden, context, w_attn_out, ln_gain, w_in, w_out, alive_mask)
    leaf_index = jnp.minimum(accepted_leaf, tree_size - 1)
    leaf_onehot = (jnp.arange(tree_width, dtype=jnp.int32)[None, :] == leaf_index[:, None]).astype(
        jnp.float32
    )
    path = jnp.einsum("ri,rij->rj", leaf_onehot, ancestors, precision=lax.Precision.HIGHEST)
    select = (
        path[:, None, :]
        * (depth[:, None, :] == jnp.arange(tree_width, dtype=jnp.int32)[None, :, None]).astype(
            jnp.float32
        )
    ).astype(jnp.bfloat16)
    kept_keys = jnp.einsum(
        "rkj,rjd->rkd",
        select,
        key_rot.reshape(requests, tree_width, width),
        preferred_element_type=jnp.float32,
    )
    kept_values = jnp.einsum(
        "rkj,rjd->rkd",
        select,
        draft_value.reshape(requests, tree_width, width),
        preferred_element_type=jnp.float32,
    )
    return (
        layer_out,
        kept_keys.reshape(rows, width).astype(jnp.bfloat16),
        kept_values.reshape(rows, width).astype(jnp.bfloat16),
    )


def solution(mesh):
    placed = (
        P("req", None),
        P("req", None),
        P("req", None),
        P("req", None),
        P("req", None, None),
        P("req", None, None),
        P("req", None),
        P("req"),
        P("req"),
        P("req", None),
        P("req"),
        P("req"),
        P(),
        P(),
        P(),
        P(),
    )
    return jax.shard_map(
        local,
        mesh=mesh,
        in_specs=placed,
        out_specs=(P("req", None), P("req", None), P("req", None)),
        check_vma=False,
    )
```
